256 devices in a mesh: pipe: 2 (over core), seq: 4 (over x), tensor: 32 (over z, y).
Axes of the slice: x: 4, y: 4, z: 8, core: 2. Of those that a mesh axis runs over, the one named last changes fastest.
Arguments:
- token_ids: int32 [2, 768], P(None, 'seq'), may hold values from 0 to 511
- embed_table: bfloat16 [512, 8192], P(None, 'tensor'), may hold values from -24 to 24
- in_proj: bfloat16 [2, 8192, 3, 4096], P('pipe', None, None, 'tensor'), may hold values from -0.0625 to 0.0625
- feat_taps: float32 [2, 3, 3, 4096], P('pipe', None, None, 'tensor'), may hold values from -3 to 3
- se_taps: float32 [7, 4096], P(None, 'tensor'), may hold values from -2 to 2
- mr_taps: float32 [128, 4096], P(None, 'tensor'), may hold values from -0.6 to 0.6
- out_proj: bfloat16 [2, 4096, 8192], P('pipe', 'tensor'), may hold values from -0.1875 to 0.1875
- norm_gain: bfloat16 [2, 8192], P('pipe', 'tensor'), may hold values from 0.25 to 1.75
Outputs:
- segment_out: bfloat16 [2, 2, 768, 8192], P('pipe', None, 'seq', 'tensor')
The draws below stay inside these ranges and needn't reach their ends.
All inputs are finite; a program needn't handle non-finite values.
Results may differ from the reference program's by a relative error of at most 0.023.
Values may be sent and summed in bfloat16 or wider, within the bound.
No kernel may reach another device: no remote copies, remote signals or barrier semaphores. Data moves between devices by JAX's collectives and lax.ppermute only.
A program may use at most 64 MiB of HBM per device.

```python
import math
import jax
import jax.numpy as jnp
from jax import lax

D = 8192
VOCAB = 512
CH = 4096
KL = 128
KS = 7
KF = 3
SEGMENTS = 2
SLICES = 2
SEQLEN = 768
N_TENSOR = 32


def draw_embed_table(key, part):
    key_base, key_rows, key_cols = jax.random.split(key, 3)
    col_scale = jnp.exp(jax.random.uniform(key_cols, (1, D), jnp.float32, math.log(0.5), math.log(2.0)))
    normal_part = jnp.clip(jax.random.normal(key_base, (VOCAB, D), jnp.float32), -4.0, 4.0)
    row_scale = jnp.exp(jax.random.uniform(key_rows, (VOCAB, 1), jnp.float32, math.log(0.3), math.log(3.0)))
    return (normal_part * row_scale * col_scale).astype(jnp.bfloat16)


def draw_mr_taps(key, part):
    key_taps, key_rate = jax.random.split(key, 2)
    decay_rate = jnp.exp(jax.random.uniform(key_rate, (1, CH), jnp.float32, math.log(1.0 / 600.0), math.log(1.0 / 25.0)))
    normal_part = jnp.clip(jax.random.normal(key_taps, (KL, CH), jnp.float32), -4.0, 4.0)
    positions = jnp.arange(KL, dtype=jnp.float32)[:, None]
    return (0.15 * normal_part * jnp.exp(-decay_rate * positions)).astype(jnp.float32)


def place_ends(result, stream_key, least, top_value):
    longest = result.shape.index(max(result.shape))
    spots = []
    for shift in (0, 1):
        where = [jax.random.randint(jax.random.fold_in(stream_key, axis), (), 0, length) for axis, length in enumerate(result.shape)]
        where[longest] = (where[longest] + shift) % result.shape[longest]
        spots.append(tuple(where))
    return result.at[spots[0]].set(least).at[spots[1]].set(top_value)


def strengthened(array, stream_key, source, target, shards_of, factor):
    owner, partner = [(jnp.arange(array.shape[dim]) // (array.shape[dim] // shards_of)).reshape([-1 if axis == dim else 1 for axis in range(array.ndim)]) for dim in (source, target)]
    chosen = jax.random.permutation(stream_key, shards_of)[partner]
    strong = (owner == chosen) | (owner == (partner + shards_of // 2) % shards_of)
    return jnp.where(strong, factor * array, array)


def level_of(rng, shape, cuts, smallest, high):
    def one(dim, blocks):
        heights = jax.random.uniform(jax.random.fold_in(jax.random.fold_in(rng, 6), dim), (blocks,), jnp.float32, smallest / len(cuts), high / len(cuts))
        return jnp.repeat(jnp.exp(heights), shape[dim] // blocks).reshape((-1,) + (1,) * (len(shape) - dim - 1))

    factor_of = one(*cuts[0])
    for cut in cuts[1:]:
        factor_of = factor_of * one(*cut)
    return factor_of


def gaussian(own_key, extent, scale, bound, shards=(), kind=jnp.bfloat16):
    factor_of = level_of(own_key, extent, shards, -0.22, 0.18) if shards else 1.0
    array = jax.random.normal(own_key, extent, jnp.float32) * scale * factor_of
    return jnp.minimum(jnp.maximum(array, -bound), bound).astype(kind)


def gaussian_with(own_key, extent, deviation, bound, cuts, heavy, held_as=jnp.bfloat16):
    drawn = deviation * jax.random.normal(own_key, extent, jnp.float32)
    if cuts:
        drawn = drawn * level_of(own_key, extent, cuts, -0.22, 0.18)
    return jnp.clip(strengthened(drawn, jax.random.fold_in(own_key, 3), *heavy), -bound, bound).astype(held_as)


def setup_inputs(seed: int = 0) -> dict:
    seeds = jax.random.split(jax.random.key(seed), 9)
    token_ids = place_ends(jax.random.randint(seeds[0], (SLICES, SEQLEN), 0, VOCAB), jax.random.fold_in(seeds[0], 1), 0, VOCAB - 1).astype(jnp.int32)
    embed_table = draw_embed_table(jax.random.fold_in(seeds[8], 71), 0)
    in_proj = gaussian(seeds[2], (SEGMENTS, D, 3, CH), D ** -0.5, 0.0625, ((0, 2), (3, 32)))
    feat_taps = gaussian(seeds[3], (SEGMENTS, KF, 3, CH), 0.6, 3.0, ((0, 2), (3, 32)), jnp.float32)
    se_taps = gaussian(seeds[4], (KS, CH), 0.4, 2.0, ((1, 32),), jnp.float32)
    mr_taps = draw_mr_taps(jax.random.fold_in(seeds[8], 71), 0)
    out_proj = gaussian_with(seeds[6], (SEGMENTS, CH, D), CH ** -0.5, 0.1875, ((0, 2), (1, 32)), (1, 2, 32, 2.75))
    norm_gain = jnp.clip(1.0 + 0.15 * jax.random.normal(seeds[7], (SEGMENTS, D), jnp.float32), 0.25, 1.75).astype(jnp.bfloat16)
    return dict(token_ids=token_ids, embed_table=embed_table, in_proj=in_proj, feat_taps=feat_taps, se_taps=se_taps, mr_taps=mr_taps, out_proj=out_proj, norm_gain=norm_gain)


epsilon = 1e-06

def hyena_layer(stream_in, in_weights, feat_weights, long_taps, out_weights, gain_row):
    window = stream_in.shape[0]
    values = stream_in.astype(jnp.float32)
    inv_rms = lax.rsqrt(lax.optimization_barrier(jnp.mean(values * values, axis=1, keepdims=True)) + epsilon)
    normed = (values * inv_rms * gain_row.astype(jnp.float32)[None, :]).astype(jnp.bfloat16)
    projected = jnp.dot(normed, in_weights.reshape(D, 3 * CH), preferred_element_type=jnp.float32).astype(jnp.bfloat16)
    raw_padded = jnp.pad(projected.astype(jnp.float32), ((KF - 1, 0), (0, 0)))
    feat_flat = feat_weights.reshape(KF, 3 * CH).astype(jnp.float32)
    featured = jnp.zeros((window, 3 * CH), jnp.float32)
    for tap_index in range(KF):
        featured = featured + feat_flat[tap_index][None, :] * raw_padded[KF - 1 - tap_index:KF - 1 - tap_index + window]
    q_feat = featured[:, :CH]
    gated_kv = featured[:, CH:2 * CH] * featured[:, 2 * CH:]
    gated_pad = jnp.pad(gated_kv, ((KL - 1, 0), (0, 0)))

    def add_tap(tap_index, running):
        shifted = lax.dynamic_slice_in_dim(gated_pad, KL - 1 - tap_index, window, 0)
        return running + long_taps[tap_index][None, :] * shifted
    filtered = lax.fori_loop(0, KL, add_tap, jnp.zeros((window, CH), jnp.float32))
    y_out = (q_feat * filtered).astype(jnp.bfloat16)
    group = CH // N_TENSOR
    y_groups = jnp.transpose(y_out.reshape(window, N_TENSOR, group), (1, 0, 2))
    w_groups = out_weights.reshape(N_TENSOR, group, D)

    def add_group(running, pair):
        part = jnp.dot(pair[0], pair[1], preferred_element_type=jnp.float32).astype(jnp.bfloat16)
        part = lax.optimization_barrier(part)
        return (running + part.astype(jnp.float32), None)
    mixed, _ = lax.scan(add_group, jnp.zeros((window, D), jnp.float32), (y_groups, w_groups))
    return (values + mixed).astype(jnp.bfloat16)

def reference(token_ids, embed_table, in_proj, feat_taps, se_taps, mr_taps, out_proj, norm_gain):
    flat_ids = token_ids.reshape(-1).astype(jnp.int32)
    embedded = jnp.take(embed_table, flat_ids, axis=0)
    se_full = jnp.concatenate([se_taps.astype(jnp.float32), jnp.zeros((KL - KS, CH), jnp.float32)], axis=0)
    first_out = hyena_layer(embedded, in_proj[0], feat_taps[0], se_full, out_proj[0], norm_gain[0])
    second_out = hyena_layer(first_out, in_proj[1], feat_taps[1], mr_taps.astype(jnp.float32), out_proj[1], norm_gain[1])
    stacked = jnp.stack([first_out, second_out], axis=0)
    return stacked.reshape(SEGMENTS, SLICES, SEQLEN, D)
```

```python
import jax
import jax.numpy as jnp
from jax import lax
from jax.sharding import PartitionSpec as P

VOCAB = 512
KL = 128
KS = 7
KF = 3
HALO = KL + KF - 2


epsilon = 1e-06


def swapped(value):
    return lax.ppermute(value, "pipe", [(0, 1), (1, 0)])


def of_section(core, own, other, section):
    return jnp.where(core == section, own, other)


def relaid_out_proj(w_down):
    n_t = lax.axis_size("tensor")
    chan_local, width = w_down.shape
    blocks = w_down.reshape(chan_local, n_t, width // n_t)
    moved = lax.all_to_all(blocks, "tensor", 1, 0, tiled=True)
    return moved.reshape(n_t * chan_local, width // n_t)


def section_step(x_in, w_in, feat, long_taps, w_out, gain):
    rows = x_in.shape[0]
    chan_local = w_in.shape[1] // 3
    aug = jnp.concatenate([x_in, gain.reshape(1, -1).astype(x_in.dtype)], axis=0)
    full = lax.all_gather(aug, "tensor", axis=1, tiled=True)
    values = full[:rows].astype(jnp.float32)
    gain_all = full[rows].astype(jnp.float32)
    inv_rms = lax.rsqrt(jnp.mean(values * values, axis=1, keepdims=True) + epsilon)
    normed = (values * inv_rms * gain_all[None, :]).astype(jnp.bfloat16)
    projected = jnp.dot(normed, w_in, preferred_element_type=jnp.float32).astype(jnp.bfloat16)

    blocks = lax.axis_size("pipe") * lax.axis_size("seq")
    kv_tail = projected[rows - HALO :, chan_local:]
    q_tail = projected[rows - (KF - 1) :, :chan_local]
    kv_prev, q_prev = lax.ppermute(
        (kv_tail, q_tail), ("pipe", "seq"), [(b, b + 1) for b in range(blocks - 1)]
    )

    q_all = jnp.concatenate([q_prev, projected[:, :chan_local]], axis=0).astype(jnp.float32)
    kv_all = jnp.concatenate([kv_prev, projected[:, chan_local:]], axis=0).astype(jnp.float32)
    q_taps = feat[:, 0, :]
    kv_taps = feat[:, 1:, :].reshape(KF, 2 * chan_local)
    kv_span = KL - 1 + rows
    q_feat = jnp.zeros((rows, chan_local), jnp.float32)
    kv_feat = jnp.zeros((kv_span, 2 * chan_local), jnp.float32)
    for tap_index in range(KF):
        offset = KF - 1 - tap_index
        q_feat = q_feat + q_taps[tap_index] * q_all[offset : offset + rows]
        kv_feat = kv_feat + kv_taps[tap_index] * kv_all[offset : offset + kv_span]
    gated_kv = kv_feat[:, :chan_local] * kv_feat[:, chan_local:]

    def add_tap(tap_index, running):
        shifted = lax.dynamic_slice_in_dim(gated_kv, KL - 1 - tap_index, rows, 0)
        return running + long_taps[tap_index] * shifted

    filtered = lax.fori_loop(0, KL, add_tap, jnp.zeros_like(q_feat))
    y_out = (q_feat * filtered).astype(jnp.bfloat16)
    y_full = lax.all_gather(y_out, "tensor", axis=1, tiled=True)
    mixed = jnp.dot(y_full, w_out, preferred_element_type=jnp.float32)
    return (x_in.astype(jnp.float32) + mixed).astype(jnp.bfloat16)


def local(token_ids, embed_table, in_proj, feat_taps, se_taps, mr_taps, out_proj, norm_gain):
    core = lax.axis_index("pipe")

    w_own = in_proj[0].reshape(in_proj.shape[1], -1)
    feat_own = feat_taps[0]
    gain_own = norm_gain[0]
    wt_own = relaid_out_proj(out_proj[0])
    w_other, feat_other, gain_other, wt_other = swapped((w_own, feat_own, gain_own, wt_own))

    padded_se = jnp.concatenate(
        [se_taps, jnp.zeros((KL - KS, se_taps.shape[1]), jnp.float32)], axis=0
    )
    filters = (padded_se, mr_taps)

    ids = lax.dynamic_index_in_dim(token_ids, core, 0, keepdims=False)
    vocab_ids = jnp.arange(VOCAB, dtype=jnp.int32)
    one_hot = (ids[:, None] == vocab_ids[None, :]).astype(jnp.bfloat16)
    current = jnp.dot(one_hot, embed_table, preferred_element_type=jnp.float32).astype(
        jnp.bfloat16
    )

    results = []
    for section in range(2):
        current = section_step(
            current,
            of_section(core, w_own, w_other, section),
            of_section(core, feat_own, feat_other, section),
            filters[section],
            of_section(core, wt_own, wt_other, section),
            of_section(core, gain_own, gain_other, section),
        )
        results.append(current)

    first_mine, second_mine = results
    second_slice_of_first = lax.ppermute(first_mine, "pipe", [(1, 0)])
    first_slice_of_second = lax.ppermute(second_mine, "pipe", [(0, 1)])
    lead = core == 0
    slice_zero = jnp.where(lead, first_mine, first_slice_of_second)
    slice_one = jnp.where(lead, second_slice_of_first, second_mine)
    return jnp.stack([slice_zero, slice_one], axis=0)[None]


def solution(mesh):
    return jax.shard_map(
        local,
        mesh=mesh,
        in_specs=(
            P(None, "seq"),
            P(None, "tensor"),
            P("pipe", None, None, "tensor"),
            P("pipe", None, None, "tensor"),
            P(None, "tensor"),
            P(None, "tensor"),
            P("pipe", "tensor", None),
            P("pipe", "tensor"),
        ),
        out_specs=P("pipe", None, "seq", "tensor"),
        check_vma=False,
    )
```

```python
import jax
import jax.numpy as jnp
from jax import lax
from jax.sharding import PartitionSpec as P

VOCAB = 512
KL = 128
KS = 7
KF = 3
HALO = KL + KF - 2
TY = 4


epsilon = 1e-06


def swapped(value):
    return lax.ppermute(value, "pipe", [(0, 1), (1, 0)])


def of_section(core, own, other, section):
    return jnp.where(core == section, own, other)


def grid_shape():
    n_t = lax.axis_size("tensor")
    return n_t // TY, TY


def shift_pairs(shift_z, shift_y):
    n_z, n_y = grid_shape()
    return [
        (z * n_y + y, ((z + shift_z) % n_z) * n_y + (y + shift_y) % n_y)
        for z in range(n_z)
        for y in range(n_y)
    ]


def ring_gather(block):
    n_z, n_y = grid_shape()
    from_below = lax.ppermute(block, "tensor", shift_pairs(0, 1))
    from_above = lax.ppermute(block, "tensor", shift_pairs(0, -1))
    from_two = lax.ppermute(from_below, "tensor", shift_pairs(0, 1))
    column = jnp.stack([block, from_above, from_two, from_below])
    ahead, behind = {}, {}
    going_up, going_down = column, column
    for step in range(1, n_z // 2 + 1):
        going_up = lax.ppermute(going_up, "tensor", shift_pairs(1, 0))
        behind[step] = going_up
        if step < n_z - step:
            going_down = lax.ppermute(going_down, "tensor", shift_pairs(-1, 0))
            ahead[step] = going_down
    parts = [column] + [ahead[a] if a in ahead else behind[n_z - a] for a in range(1, n_z)]
    return jnp.stack(parts)


def relative_rows(weights):
    n_z, n_y = grid_shape()
    t = lax.axis_index("tensor")
    z, y = t // n_y, t % n_y
    grid = weights.reshape(n_z, n_y, -1, weights.shape[-1])
    grid = jnp.take(grid, (jnp.arange(n_z) + z) % n_z, axis=0)
    return jnp.take(grid, (jnp.arange(n_y) + y) % n_y, axis=1)


def relaid_out_proj(w_down):
    n_t = lax.axis_size("tensor")
    chan_local, width = w_down.shape
    blocks = w_down.reshape(chan_local, n_t, width // n_t)
    moved = lax.all_to_all(blocks, "tensor", 1, 0, tiled=True)
    return moved.reshape(n_t * chan_local, width // n_t)


def section_step(x_in, w_in, feat, long_taps, w_out, gain):
    rows = x_in.shape[0]
    chan_local = w_in.shape[-1] // 3
    aug = jnp.concatenate([x_in, gain.reshape(1, -1).astype(x_in.dtype)], axis=0)
    full = ring_gather(aug)
    values = full[:, :, :rows].astype(jnp.float32)
    gain_all = full[:, :, rows:].astype(jnp.float32)
    inv_rms = lax.rsqrt(jnp.mean(values * values, axis=(0, 1, 3), keepdims=True) + epsilon)
    normed = (values * inv_rms * gain_all).astype(jnp.bfloat16)
    projected = jnp.einsum(
        "abrf,abfk->rk", normed, w_in, preferred_element_type=jnp.float32
    ).astype(jnp.bfloat16)

    blocks = lax.axis_size("pipe") * lax.axis_size("seq")
    kv_tail = projected[rows - HALO :, chan_local:]
    q_tail = projected[rows - (KF - 1) :, :chan_local]
    kv_prev, q_prev = lax.ppermute(
        (kv_tail, q_tail), ("pipe", "seq"), [(b, b + 1) for b in range(blocks - 1)]
    )

    q_all = jnp.concatenate([q_prev, projected[:, :chan_local]], axis=0).astype(jnp.float32)
    kv_all = jnp.concatenate([kv_prev, projected[:, chan_local:]], axis=0).astype(jnp.float32)
    q_taps = feat[:, 0, :]
    kv_taps = feat[:, 1:, :].reshape(KF, 2 * chan_local)
    kv_span = KL - 1 + rows
    q_feat = jnp.zeros((rows, chan_local), jnp.float32)
    kv_feat = jnp.zeros((kv_span, 2 * chan_local), jnp.float32)
    for tap_index in range(KF):
        offset = KF - 1 - tap_index
        q_feat = q_feat + q_taps[tap_index] * q_all[offset : offset + rows]
        kv_feat = kv_feat + kv_taps[tap_index] * kv_all[offset : offset + kv_span]
    gated_kv = kv_feat[:, :chan_local] * kv_feat[:, chan_local:]

    filtered = jnp.zeros_like(q_feat)
    for tap_index in range(KL):
        start = KL - 1 - tap_index
        filtered = filtered + long_taps[tap_index] * gated_kv[start : start + rows]
    y_out = (q_feat * filtered).astype(jnp.bfloat16)
    y_full = ring_gather(y_out)
    mixed = jnp.einsum("abrc,abcd->rd", y_full, w_out, preferred_element_type=jnp.float32)
    return (x_in.astype(jnp.float32) + mixed).astype(jnp.bfloat16)


def local(token_ids, embed_table, in_proj, feat_taps, se_taps, mr_taps, out_proj, norm_gain):
    core = lax.axis_index("pipe")

    w_own = relative_rows(in_proj[0].reshape(in_proj.shape[1], -1))
    feat_own = feat_taps[0]
    gain_own = norm_gain[0]
    wt_own = relative_rows(relaid_out_proj(out_proj[0]))
    w_other, feat_other, gain_other, wt_other = swapped((w_own, feat_own, gain_own, wt_own))

    padded_se = jnp.concatenate(
        [se_taps, jnp.zeros((KL - KS, se_taps.shape[1]), jnp.float32)], axis=0
    )
    filters = (padded_se, mr_taps)

    ids = lax.dynamic_index_in_dim(token_ids, core, 0, keepdims=False)
    vocab_ids = jnp.arange(VOCAB, dtype=jnp.int32)
    one_hot = (ids[:, None] == vocab_ids[None, :]).astype(jnp.bfloat16)
    current = jnp.dot(one_hot, embed_table, preferred_element_type=jnp.float32).astype(
        jnp.bfloat16
    )

    results = []
    for section in range(2):
        current = section_step(
            current,
            of_section(core, w_own, w_other, section),
            of_section(core, feat_own, feat_other, section),
            filters[section],
            of_section(core, wt_own, wt_other, section),
            of_section(core, gain_own, gain_other, section),
        )
        results.append(current)

    first_mine, second_mine = results
    second_slice_of_first = lax.ppermute(first_mine, "pipe", [(1, 0)])
    first_slice_of_second = lax.ppermute(second_mine, "pipe", [(0, 1)])
    lead = core == 0
    slice_zero = jnp.where(lead, first_mine, first_slice_of_second)
    slice_one = jnp.where(lead, second_slice_of_first, second_mine)
    return jnp.stack([slice_zero, slice_one], axis=0)[None]


def solution(mesh):
    return jax.shard_map(
        local,
        mesh=mesh,
        in_specs=(
            P(None, "seq"),
            P(None, "tensor"),
            P("pipe", None, None, "tensor"),
            P("pipe", None, None, "tensor"),
            P(None, "tensor"),
            P(None, "tensor"),
            P("pipe", "tensor", None),
            P("pipe", "tensor"),
        ),
        out_specs=P("pipe", None, "seq", "tensor"),
        check_vma=False,
    )
```

```python
import jax
import jax.numpy as jnp
from jax import lax
from jax.sharding import PartitionSpec as P

VOCAB = 512
KL = 128
KS = 7
KF = 3
HALO = KL + KF - 2
TY = 4


epsilon = 1e-06


def swapped(value):
    return lax.ppermute(value, "pipe", [(0, 1), (1, 0)])


def of_section(core, own, other, section):
    return jnp.where(core == section, own, other)


def grid_shape():
    n_t = lax.axis_size("tensor")
    return n_t // TY, TY


def shift_pairs(shift_z, shift_y):
    n_z, n_y = grid_shape()
    return [
        (z * n_y + y, ((z + shift_z) % n_z) * n_y + (y + shift_y) % n_y)
        for z in range(n_z)
        for y in range(n_y)
    ]


def ring_gather(block):
    n_z, n_y = grid_shape()
    from_below = lax.ppermute(block, "tensor", shift_pairs(0, 1))
    from_above = lax.ppermute(block, "tensor", shift_pairs(0, -1))
    from_two = lax.ppermute(from_below, "tensor", shift_pairs(0, 1))
    column = jnp.stack([block, from_above, from_two, from_below])
    ahead, behind = {}, {}
    going_up, going_down = column, column
    for step in range(1, n_z // 2 + 1):
        going_up = lax.ppermute(going_up, "tensor", shift_pairs(1, 0))
        behind[step] = going_up
        if step < n_z - step:
            going_down = lax.ppermute(going_down, "tensor", shift_pairs(-1, 0))
            ahead[step] = going_down
    parts = [column] + [ahead[a] if a in ahead else behind[n_z - a] for a in range(1, n_z)]
    return jnp.stack(parts)


def absolute_order(gathered):
    n_z, n_y = grid_shape()
    t = lax.axis_index("tensor")
    z, y = t // n_y, t % n_y
    gathered = jnp.take(gathered, (jnp.arange(n_z) - z) % n_z, axis=0)
    return jnp.take(gathered, (jnp.arange(n_y) - y) % n_y, axis=1)


def chosen_dot(use_own, spec, lhs, own, other):
    return lax.cond(
        use_own,
        lambda a, w, _: jnp.einsum(spec, a, w, preferred_element_type=jnp.float32),
        lambda a, _, w: jnp.einsum(spec, a, w, preferred_element_type=jnp.float32),
        lhs,
        own,
        other,
    )


def relaid_out_proj(w_down):
    n_t = lax.axis_size("tensor")
    chan_local, width = w_down.shape
    blocks = w_down.reshape(chan_local, n_t, width // n_t)
    moved = lax.all_to_all(blocks, "tensor", 1, 0, tiled=True)
    return moved.reshape(n_t * chan_local, width // n_t)


def section_step(x_in, use_own, w_in, feat, long_taps, w_out, gain):
    rows = x_in.shape[0]
    n_z, n_y = grid_shape()
    chan_local = w_in[0].shape[-1]
    aug = jnp.concatenate([x_in, gain.reshape(1, -1).astype(x_in.dtype)], axis=0)
    full = absolute_order(ring_gather(aug))
    full, w_out = w_out(full)
    values = full[:, :, :rows].astype(jnp.float32)
    gain_all = full[:, :, rows:].astype(jnp.float32)
    inv_rms = lax.rsqrt(jnp.mean(values * values, axis=(0, 1, 3), keepdims=True) + epsilon)
    normed = (values * inv_rms * gain_all).astype(jnp.bfloat16)
    w_grid = [w.reshape((n_z, n_y, -1) + w.shape[1:]) for w in w_in]
    projected = chosen_dot(use_own, "abrf,abfjc->rjc", normed, *w_grid).astype(jnp.bfloat16)

    blocks = lax.axis_size("pipe") * lax.axis_size("seq")
    kv_tail = projected[rows - HALO :, 1:]
    q_tail = projected[rows - (KF - 1) :, 0]
    kv_prev, q_prev = lax.ppermute(
        (kv_tail, q_tail), ("pipe", "seq"), [(b, b + 1) for b in range(blocks - 1)]
    )

    q_all = jnp.concatenate([q_prev, projected[:, 0]], axis=0).astype(jnp.float32)
    kv_all = jnp.concatenate([kv_prev, projected[:, 1:]], axis=0).astype(jnp.float32)
    q_taps = feat[:, 0, :]
    kv_taps = feat[:, 1:, :]
    kv_span = KL - 1 + rows
    q_feat = jnp.zeros((rows, chan_local), jnp.float32)
    kv_feat = jnp.zeros((kv_span, 2, chan_local), jnp.float32)
    for tap_index in range(KF):
        offset = KF - 1 - tap_index
        q_feat = q_feat + q_taps[tap_index] * q_all[offset : offset + rows]
        kv_feat = kv_feat + kv_taps[tap_index] * kv_all[offset : offset + kv_span]
    gated_kv = kv_feat[:, 0] * kv_feat[:, 1]

    filtered = jnp.zeros_like(q_feat)
    for tap_index in range(KL):
        start = KL - 1 - tap_index
        filtered = filtered + long_taps[tap_index] * gated_kv[start : start + rows]
    y_out = (q_feat * filtered).astype(jnp.bfloat16)
    y_full = absolute_order(ring_gather(y_out))
    w_out_grid = [w.reshape((n_z, n_y, -1, w.shape[-1])) for w in w_out]
    mixed = chosen_dot(use_own, "abrc,abcd->rd", y_full, *w_out_grid)
    return (x_in.astype(jnp.float32) + mixed).astype(jnp.bfloat16)


def local(token_ids, embed_table, in_proj, feat_taps, se_taps, mr_taps, out_proj, norm_gain):
    core = lax.axis_index("pipe")

    w_own = in_proj[0]
    feat_own = feat_taps[0]
    gain_own = norm_gain[0]
    w_other, feat_other, gain_other = swapped((w_own, feat_own, gain_own))

    def out_weights_after(full):
        full, w_down = lax.optimization_barrier((full, out_proj[0]))
        wt_own = relaid_out_proj(w_down)
        return full, (wt_own, swapped(wt_own))

    padded_se = jnp.concatenate(
        [se_taps, jnp.zeros((KL - KS, se_taps.shape[1]), jnp.float32)], axis=0
    )
    filters = (padded_se, mr_taps)

    ids = lax.dynamic_index_in_dim(token_ids, core, 0, keepdims=False)
    vocab_ids = jnp.arange(VOCAB, dtype=jnp.int32)
    one_hot = (ids[:, None] == vocab_ids[None, :]).astype(jnp.bfloat16)
    current = jnp.dot(one_hot, embed_table, preferred_element_type=jnp.float32).astype(
        jnp.bfloat16
    )

    results = []
    relaid = []

    def relaid_once(full):
        if relaid:
            return full, relaid
        full, pair = out_weights_after(full)
        relaid.extend(pair)
        return full, pair

    for section in range(2):
        current = section_step(
            current,
            core == section,
            (w_own, w_other),
            of_section(core, feat_own, feat_other, section),
            filters[section],
            relaid_once,
            of_section(core, gain_own, gain_other, section),
        )
        results.append(current)

    first_mine, second_mine = results
    second_slice_of_first = lax.ppermute(first_mine, "pipe", [(1, 0)])
    first_slice_of_second = lax.ppermute(second_mine, "pipe", [(0, 1)])
    lead = core == 0
    slice_zero = jnp.where(lead, first_mine, first_slice_of_second)
    slice_one = jnp.where(lead, second_slice_of_first, second_mine)
    return jnp.stack([slice_zero, slice_one], axis=0)[None]


def solution(mesh):
    return jax.shard_map(
        local,
        mesh=mesh,
        in_specs=(
            P(None, "seq"),
            P(None, "tensor"),
            P("pipe", None, None, "tensor"),
            P("pipe", None, None, "tensor"),
            P(None, "tensor"),
            P(None, "tensor"),
            P("pipe", "tensor", None),
            P("pipe", "tensor"),
        ),
        out_specs=P("pipe", None, "seq", "tensor"),
        check_vma=False,
    )
```

```python
import jax
import jax.numpy as jnp
from jax import lax
from jax.sharding import PartitionSpec as P

VOCAB = 512
KL = 128
KS = 7
KF = 3
HALO = KL + KF - 2
TY = 4


epsilon = 1e-06


def swapped(value):
    return lax.ppermute(value, "pipe", [(0, 1), (1, 0)])


def of_section(core, own, other, section):
    return jnp.where(core == section, own, other)


def grid_shape():
    n_t = lax.axis_size("tensor")
    return n_t // TY, TY


def shift_pairs(shift_z, shift_y):
    n_z, n_y = grid_shape()
    return [
        (z * n_y + y, ((z + shift_z) % n_z) * n_y + (y + shift_y) % n_y)
        for z in range(n_z)
        for y in range(n_y)
    ]


def ring_gather(block):
    n_z, n_y = grid_shape()
    from_below = lax.ppermute(block, "tensor", shift_pairs(0, 1))
    from_above = lax.ppermute(block, "tensor", shift_pairs(0, -1))
    from_two = lax.ppermute(block, "tensor", shift_pairs(0, 2))
    column = jnp.stack([block, from_above, from_two, from_below])
    ahead, behind = {}, {}
    going_up, going_down = column, column
    for step in range(1, n_z // 2 + 1):
        going_up = lax.ppermute(going_up, "tensor", shift_pairs(1, 0))
        behind[step] = going_up
        if step < n_z - step:
            going_down = lax.ppermute(going_down, "tensor", shift_pairs(-1, 0))
            ahead[step] = going_down
    parts = [column] + [ahead[a] if a in ahead else behind[n_z - a] for a in range(1, n_z)]
    return jnp.stack(parts)


def absolute_order(gathered):
    n_z, n_y = grid_shape()
    t = lax.axis_index("tensor")
    z, y = t // n_y, t % n_y
    gathered = jnp.take(gathered, (jnp.arange(n_z) - z) % n_z, axis=0)
    return jnp.take(gathered, (jnp.arange(n_y) - y) % n_y, axis=1)


def chosen_dot(use_own, spec, lhs, own, other):
    return lax.cond(
        use_own,
        lambda a, w, _: jnp.einsum(spec, a, w, preferred_element_type=jnp.float32),
        lambda a, _, w: jnp.einsum(spec, a, w, preferred_element_type=jnp.float32),
        lhs,
        own,
        other,
    )


def relaid_out_proj(w_down):
    n_t = lax.axis_size("tensor")
    chan_local, width = w_down.shape
    blocks = w_down.reshape(chan_local, n_t, width // n_t)
    moved = lax.all_to_all(blocks, "tensor", 1, 0, tiled=True)
    return moved.reshape(n_t * chan_local, width // n_t)


def section_step(x_in, use_own, w_in, feat, long_taps, w_out, gain):
    rows = x_in.shape[0]
    n_z, n_y = grid_shape()
    chan_local = w_in[0].shape[-1]
    aug = jnp.concatenate([x_in, gain.reshape(1, -1).astype(x_in.dtype)], axis=0)
    full, w_out = w_out(ring_gather(aug))
    full = absolute_order(full)
    values = full[:, :, :rows].astype(jnp.float32)
    gain_all = full[:, :, rows:].astype(jnp.float32)
    inv_rms = lax.rsqrt(jnp.mean(values * values, axis=(0, 1, 3), keepdims=True) + epsilon)
    normed = (values * inv_rms * gain_all).astype(jnp.bfloat16)
    w_grid = [w.reshape((n_z, n_y, -1) + w.shape[1:]) for w in w_in]
    projected = chosen_dot(use_own, "abrf,abfjc->rjc", normed, *w_grid).astype(jnp.bfloat16)

    blocks = lax.axis_size("pipe") * lax.axis_size("seq")
    tail = lax.ppermute(
        projected[rows - HALO :], ("pipe", "seq"), [(b, b + 1) for b in range(blocks - 1)]
    )
    kv_prev = tail[:, 1:]
    q_prev = tail[HALO - (KF - 1) :, 0]

    q_all = jnp.concatenate([q_prev, projected[:, 0]], axis=0).astype(jnp.float32)
    kv_all = jnp.concatenate([kv_prev, projected[:, 1:]], axis=0).astype(jnp.float32)
    q_taps = feat[:, 0, :]
    kv_taps = feat[:, 1:, :]
    kv_span = KL - 1 + rows
    q_feat = jnp.zeros((rows, chan_local), jnp.float32)
    kv_feat = jnp.zeros((kv_span, 2, chan_local), jnp.float32)
    for tap_index in range(KF):
        offset = KF - 1 - tap_index
        q_feat = q_feat + q_taps[tap_index] * q_all[offset : offset + rows]
        kv_feat = kv_feat + kv_taps[tap_index] * kv_all[offset : offset + kv_span]
    gated_kv = kv_feat[:, 0] * kv_feat[:, 1]

    filtered = jnp.zeros_like(q_feat)
    for tap_index in range(KL):
        start = KL - 1 - tap_index
        filtered = filtered + long_taps[tap_index] * gated_kv[start : start + rows]
    y_out = (q_feat * filtered).astype(jnp.bfloat16)
    y_full = absolute_order(ring_gather(y_out))
    w_out_grid = [w.reshape((n_z, n_y, -1, w.shape[-1])) for w in w_out]
    mixed = chosen_dot(use_own, "abrc,abcd->rd", y_full, *w_out_grid)
    return (x_in.astype(jnp.float32) + mixed).astype(jnp.bfloat16)


def local(token_ids, embed_table, in_proj, feat_taps, se_taps, mr_taps, out_proj, norm_gain):
    core = lax.axis_index("pipe")

    w_own = in_proj[0]
    feat_own = feat_taps[0]
    gain_own = norm_gain[0]
    w_other, feat_other, gain_other = swapped((w_own, feat_own, gain_own))

    def out_weights_after(full):
        full, w_down = lax.optimization_barrier((full, out_proj[0]))
        wt_own = relaid_out_proj(w_down)
        return full, (wt_own, swapped(wt_own))

    padded_se = jnp.concatenate(
        [se_taps, jnp.zeros((KL - KS, se_taps.shape[1]), jnp.float32)], axis=0
    )
    filters = (padded_se, mr_taps)

    ids = lax.dynamic_index_in_dim(token_ids, core, 0, keepdims=False)
    vocab_ids = jnp.arange(VOCAB, dtype=jnp.int32)
    one_hot = (ids[:, None] == vocab_ids[None, :]).astype(jnp.bfloat16)
    current = jnp.dot(one_hot, embed_table, preferred_element_type=jnp.float32).astype(
        jnp.bfloat16
    )

    results = []
    relaid = []

    def relaid_once(full):
        if relaid:
            return full, relaid
        full, pair = out_weights_after(full)
        relaid.extend(pair)
        return full, pair

    for section in range(2):
        current = section_step(
            current,
            core == section,
            (w_own, w_other),
            of_section(core, feat_own, feat_other, section),
            filters[section],
            relaid_once,
            of_section(core, gain_own, gain_other, section),
        )
        results.append(current)

    first_mine, second_mine = results
    second_slice_of_first = lax.ppermute(first_mine, "pipe", [(1, 0)])
    first_slice_of_second = lax.ppermute(second_mine, "pipe", [(0, 1)])
    lead = core == 0
    slice_zero = jnp.where(lead, first_mine, first_slice_of_second)
    slice_one = jnp.where(lead, second_slice_of_first, second_mine)
    return jnp.stack([slice_zero, slice_one], axis=0)[None]


def solution(mesh):
    return jax.shard_map(
        local,
        mesh=mesh,
        in_specs=(
            P(None, "seq"),
            P(None, "tensor"),
            P("pipe", None, None, "tensor"),
            P("pipe", None, None, "tensor"),
            P(None, "tensor"),
            P(None, "tensor"),
            P("pipe", "tensor", None),
            P("pipe", "tensor"),
        ),
        out_specs=P("pipe", None, "seq", "tensor"),
        check_vma=False,
    )
```

```python
import jax
import jax.numpy as jnp
from jax import lax
from jax.sharding import PartitionSpec as P

VOCAB = 512
KL = 128
KS = 7
KF = 3
HALO = KL + KF - 2
TY = 4


epsilon = 1e-06


def swapped(value):
    return lax.ppermute(value, "pipe", [(0, 1), (1, 0)])


def of_section(core, own, other, section):
    return jnp.where(core == section, own, other)


def grid_shape():
    n_t = lax.axis_size("tensor")
    return n_t // TY, TY


def shift_pairs(shift_z, shift_y):
    n_z, n_y = grid_shape()
    return [
        (z * n_y + y, ((z + shift_z) % n_z) * n_y + (y + shift_y) % n_y)
        for z in range(n_z)
        for y in range(n_y)
    ]


def ring_gather(block, two_rounds=False):
    n_z, n_y = grid_shape()
    from_below = lax.ppermute(block, "tensor", shift_pairs(0, 1))
    from_above = lax.ppermute(block, "tensor", shift_pairs(0, -1))
    from_two = lax.ppermute(block, "tensor", shift_pairs(0, 2))
    column = jnp.stack([block, from_above, from_two, from_below])
    if two_rounds and n_z == 8:
        near = {a: lax.ppermute(column, "tensor", shift_pairs(-a, 0)) for a in (1, 2, -1, -2)}
        lower = lax.ppermute(jnp.stack([near[-1], near[-2]]), "tensor", shift_pairs(2, 0))
        upper = lax.ppermute(near[1], "tensor", shift_pairs(-2, 0))
        parts = [column, near[1], near[2], upper, lower[1], lower[0], near[-2], near[-1]]
        return jnp.stack(parts)
    ahead, behind = {}, {}
    going_up, going_down = column, column
    for step in range(1, n_z // 2 + 1):
        going_up = lax.ppermute(going_up, "tensor", shift_pairs(1, 0))
        behind[step] = going_up
        if step < n_z - step:
            going_down = lax.ppermute(going_down, "tensor", shift_pairs(-1, 0))
            ahead[step] = going_down
    parts = [column] + [ahead[a] if a in ahead else behind[n_z - a] for a in range(1, n_z)]
    return jnp.stack(parts)


def absolute_order(gathered):
    n_z, n_y = grid_shape()
    t = lax.axis_index("tensor")
    z, y = t // n_y, t % n_y
    slots = jnp.arange(n_z * n_y)
    source = ((slots // n_y - z) % n_z) * n_y + (slots % n_y - y) % n_y
    flat = gathered.reshape((n_z * n_y,) + gathered.shape[2:])
    picked = jnp.take(flat, source, axis=0, mode="clip")
    return picked.reshape(gathered.shape)


def chosen_dot(use_own, spec, lhs, own, other):
    return lax.cond(
        use_own,
        lambda a, w, _: jnp.einsum(spec, a, w, preferred_element_type=jnp.float32),
        lambda a, _, w: jnp.einsum(spec, a, w, preferred_element_type=jnp.float32),
        lhs,
        own,
        other,
    )


def relaid_out_proj(w_down):
    n_t = lax.axis_size("tensor")
    chan_local, width = w_down.shape
    blocks = w_down.reshape(chan_local, n_t, width // n_t)
    moved = lax.all_to_all(blocks, "tensor", 1, 0, tiled=True)
    return moved.reshape(n_t * chan_local, width // n_t)


def section_step(x_in, use_own, w_in, feat, long_taps, w_out, gain):
    rows = x_in.shape[0]
    n_z, n_y = grid_shape()
    chan_local = w_in[0].shape[-1]
    aug = jnp.concatenate([x_in, gain.reshape(1, -1).astype(x_in.dtype)], axis=0)
    full, w_out = w_out(ring_gather(aug))
    full = absolute_order(full)
    values = full[:, :, :rows].astype(jnp.float32)
    gain_all = full[:, :, rows:].astype(jnp.float32)
    inv_rms = lax.rsqrt(jnp.mean(values * values, axis=(0, 1, 3), keepdims=True) + epsilon)
    normed = (values * inv_rms * gain_all).astype(jnp.bfloat16)
    w_grid = [w.reshape((n_z, n_y, -1) + w.shape[1:]) for w in w_in]
    projected = chosen_dot(use_own, "abrf,abfjc->rjc", normed, *w_grid).astype(jnp.bfloat16)

    blocks = lax.axis_size("pipe") * lax.axis_size("seq")
    tail = lax.ppermute(
        projected[rows - HALO :], ("pipe", "seq"), [(b, b + 1) for b in range(blocks - 1)]
    )
    kv_prev = tail[:, 1:]
    q_prev = tail[HALO - (KF - 1) :, 0]

    q_all = jnp.concatenate([q_prev, projected[:, 0]], axis=0).astype(jnp.float32)
    kv_all = jnp.concatenate([kv_prev, projected[:, 1:]], axis=0).astype(jnp.float32)
    q_taps = feat[:, 0, :]
    kv_taps = feat[:, 1:, :]
    kv_span = KL - 1 + rows
    q_feat = jnp.zeros((rows, chan_local), jnp.float32)
    kv_feat = jnp.zeros((kv_span, 2, chan_local), jnp.float32)
    for tap_index in range(KF):
        offset = KF - 1 - tap_index
        q_feat = q_feat + q_taps[tap_index] * q_all[offset : offset + rows]
        kv_feat = kv_feat + kv_taps[tap_index] * kv_all[offset : offset + kv_span]
    gated_kv = kv_feat[:, 0] * kv_feat[:, 1]

    filtered = jnp.zeros_like(q_feat)
    for tap_index in range(KL):
        start = KL - 1 - tap_index
        filtered = filtered + long_taps[tap_index] * gated_kv[start : start + rows]
    y_out = (q_feat * filtered).astype(jnp.bfloat16)
    y_full = absolute_order(ring_gather(y_out, two_rounds=True))
    w_out_grid = [w.reshape((n_z, n_y, -1, w.shape[-1])) for w in w_out]
    mixed = chosen_dot(use_own, "abrc,abcd->rd", y_full, *w_out_grid)
    return (x_in.astype(jnp.float32) + mixed).astype(jnp.bfloat16)


def local(token_ids, embed_table, in_proj, feat_taps, se_taps, mr_taps, out_proj, norm_gain):
    core = lax.axis_index("pipe")

    w_own = in_proj[0]
    feat_own = feat_taps[0]
    gain_own = norm_gain[0]
    w_other, feat_other, gain_other = swapped((w_own, feat_own, gain_own))

    def out_weights_after(full):
        full, w_down = lax.optimization_barrier((full, out_proj[0]))
        wt_own = relaid_out_proj(w_down)
        return full, (wt_own, swapped(wt_own))

    padded_se = jnp.concatenate(
        [se_taps, jnp.zeros((KL - KS, se_taps.shape[1]), jnp.float32)], axis=0
    )
    filters = (padded_se, mr_taps)

    ids = lax.dynamic_index_in_dim(token_ids, core, 0, keepdims=False)
    vocab_ids = jnp.arange(VOCAB, dtype=jnp.int32)
    one_hot = (ids[:, None] == vocab_ids[None, :]).astype(jnp.bfloat16)
    current = jnp.dot(one_hot, embed_table, preferred_element_type=jnp.float32).astype(
        jnp.bfloat16
    )

    results = []
    relaid = []

    def relaid_once(full):
        if relaid:
            return full, relaid
        full, pair = out_weights_after(full)
        relaid.extend(pair)
        return full, pair

    for section in range(2):
        current = section_step(
            current,
            core == section,
            (w_own, w_other),
            of_section(core, feat_own, feat_other, section),
            filters[section],
            relaid_once,
            of_section(core, gain_own, gain_other, section),
        )
        results.append(current)

    first_mine, second_mine = results
    second_slice_of_first = lax.ppermute(first_mine, "pipe", [(1, 0)])
    first_slice_of_second = lax.ppermute(second_mine, "pipe", [(0, 1)])
    lead = core == 0
    slice_zero = jnp.where(lead, first_mine, first_slice_of_second)
    slice_one = jnp.where(lead, second_slice_of_first, second_mine)
    return jnp.stack([slice_zero, slice_one], axis=0)[None]


def solution(mesh):
    return jax.shard_map(
        local,
        mesh=mesh,
        in_specs=(
            P(None, "seq"),
            P(None, "tensor"),
            P("pipe", None, None, "tensor"),
            P("pipe", None, None, "tensor"),
            P(None, "tensor"),
            P(None, "tensor"),
            P("pipe", "tensor", None),
            P("pipe", "tensor"),
        ),
        out_specs=P("pipe", None, "seq", "tensor"),
        check_vma=False,
    )
```

```python
import jax
import jax.numpy as jnp
from jax import lax
from jax.sharding import PartitionSpec as P

VOCAB = 512
KL = 128
KS = 7
KF = 3
HALO = KL + KF - 2
TY = 4


epsilon = 1e-06


def swapped(value):
    return lax.ppermute(value, "pipe", [(0, 1), (1, 0)])


def of_section(core, own, other, section):
    return jnp.where(core == section, own, other)


def grid_shape():
    n_t = lax.axis_size("tensor")
    return n_t // TY, TY


def shift_pairs(shift_z, shift_y):
    n_z, n_y = grid_shape()
    return [
        (z * n_y + y, ((z + shift_z) % n_z) * n_y + (y + shift_y) % n_y)
        for z in range(n_z)
        for y in range(n_y)
    ]


def ring_gather(block, two_rounds=False):
    n_z, n_y = grid_shape()
    from_below = lax.ppermute(block, "tensor", shift_pairs(0, 1))
    from_above = lax.ppermute(block, "tensor", shift_pairs(0, -1))
    from_two = lax.ppermute(block, "tensor", shift_pairs(0, 2))
    column = jnp.stack([block, from_above, from_two, from_below])
    if two_rounds and n_z == 8:
        near = {a: lax.ppermute(column, "tensor", shift_pairs(-a, 0)) for a in (1, 2, -1, -2)}
        lower = lax.ppermute(jnp.stack([near[-1], near[-2]]), "tensor", shift_pairs(2, 0))
        upper = lax.ppermute(near[1], "tensor", shift_pairs(-2, 0))
        parts = [column, near[1], near[2], upper, lower[1], lower[0], near[-2], near[-1]]
        return jnp.stack(parts)
    ahead, behind = {}, {}
    going_up, going_down = column, column
    for step in range(1, n_z // 2 + 1):
        going_up = lax.ppermute(going_up, "tensor", shift_pairs(1, 0))
        behind[step] = going_up
        if step < n_z - step:
            going_down = lax.ppermute(going_down, "tensor", shift_pairs(-1, 0))
            ahead[step] = going_down
    parts = [column] + [ahead[a] if a in ahead else behind[n_z - a] for a in range(1, n_z)]
    return jnp.stack(parts)


def absolute_order(gathered):
    n_z, n_y = grid_shape()
    t = lax.axis_index("tensor")
    z, y = t // n_y, t % n_y
    slots = jnp.arange(n_z * n_y)
    source = ((slots // n_y - z) % n_z) * n_y + (slots % n_y - y) % n_y
    flat = gathered.reshape((n_z * n_y,) + gathered.shape[2:])
    picked = jnp.take(flat, source, axis=0, mode="clip")
    return picked.reshape(gathered.shape)


def chosen_dot(use_own, spec, lhs, own, other):
    return lax.cond(
        use_own,
        lambda a, w, _: jnp.einsum(spec, a, w, preferred_element_type=jnp.float32),
        lambda a, _, w: jnp.einsum(spec, a, w, preferred_element_type=jnp.float32),
        lhs,
        own,
        other,
    )


def relaid_out_proj(w_down):
    n_t = lax.axis_size("tensor")
    chan_local, width = w_down.shape
    blocks = w_down.reshape(chan_local, n_t, width // n_t)
    moved = lax.all_to_all(blocks, "tensor", 1, 0, tiled=True)
    return moved.reshape(n_t * chan_local, width // n_t)


def section_step(x_in, use_own, w_in, feat, long_taps, after_gather, gain, two_rounds):
    rows = x_in.shape[0]
    n_z, n_y = grid_shape()
    chan_local = w_in[0].shape[-1]
    aug = jnp.concatenate([x_in, gain.reshape(1, -1).astype(x_in.dtype)], axis=0)
    full, w_out = after_gather(ring_gather(aug))
    full = absolute_order(full)
    values = full[:, :, :rows].astype(jnp.float32)
    gain_all = full[:, :, rows:].astype(jnp.float32)
    inv_rms = lax.rsqrt(jnp.mean(values * values, axis=(0, 1, 3), keepdims=True) + epsilon)
    normed = (values * inv_rms * gain_all).astype(jnp.bfloat16)
    w_grid = [w.reshape((n_z, n_y, -1) + w.shape[1:]) for w in w_in]
    projected = chosen_dot(use_own, "abrf,abfjc->rjc", normed, *w_grid).astype(jnp.bfloat16)

    blocks = lax.axis_size("pipe") * lax.axis_size("seq")
    tail = lax.ppermute(
        projected[rows - HALO :], ("pipe", "seq"), [(b, b + 1) for b in range(blocks - 1)]
    )
    kv_prev = tail[:, 1:]
    q_prev = tail[HALO - (KF - 1) :, 0]

    q_all = jnp.concatenate([q_prev, projected[:, 0]], axis=0).astype(jnp.float32)
    kv_all = jnp.concatenate([kv_prev, projected[:, 1:]], axis=0).astype(jnp.float32)
    q_taps = feat[:, 0, :]
    kv_taps = feat[:, 1:, :]
    kv_span = KL - 1 + rows
    q_feat = jnp.zeros((rows, chan_local), jnp.float32)
    kv_feat = jnp.zeros((kv_span, 2, chan_local), jnp.float32)
    for tap_index in range(KF):
        offset = KF - 1 - tap_index
        q_feat = q_feat + q_taps[tap_index] * q_all[offset : offset + rows]
        kv_feat = kv_feat + kv_taps[tap_index] * kv_all[offset : offset + kv_span]
    gated_kv = kv_feat[:, 0] * kv_feat[:, 1]

    filtered = jnp.zeros_like(q_feat)
    for tap_index in range(KL):
        start = KL - 1 - tap_index
        filtered = filtered + long_taps[tap_index] * gated_kv[start : start + rows]
    y_out = (q_feat * filtered).astype(jnp.bfloat16)
    y_full = absolute_order(ring_gather(y_out, two_rounds))
    w_out_grid = [w.reshape((n_z, n_y, -1, w.shape[-1])) for w in w_out]
    mixed = chosen_dot(use_own, "abrc,abcd->rd", y_full, *w_out_grid)
    return (x_in.astype(jnp.float32) + mixed).astype(jnp.bfloat16)


def local(token_ids, embed_table, in_proj, feat_taps, se_taps, mr_taps, out_proj, norm_gain):
    core = lax.axis_index("pipe")

    w_own = in_proj[0]
    feat_own = feat_taps[0]
    gain_own = norm_gain[0]
    feat_other, gain_other = swapped((feat_own, gain_own))
    w_first = lax.ppermute(w_own, "pipe", [(0, 1)])
    later = {}

    def after_first_gather(full):
        full, w_down, w_held = lax.optimization_barrier((full, out_proj[0], w_own))
        wt_own = relaid_out_proj(w_down)
        later["w"] = lax.ppermute(w_held, "pipe", [(1, 0)])
        later["wt"] = lax.ppermute(wt_own, "pipe", [(1, 0)])
        return full, (wt_own, lax.ppermute(wt_own, "pipe", [(0, 1)]))

    def after_second_gather(full):
        return full, (later["wt_own"], later["wt"])

    padded_se = jnp.concatenate(
        [se_taps, jnp.zeros((KL - KS, se_taps.shape[1]), jnp.float32)], axis=0
    )

    ids = lax.dynamic_index_in_dim(token_ids, core, 0, keepdims=False)
    vocab_ids = jnp.arange(VOCAB, dtype=jnp.int32)
    one_hot = (ids[:, None] == vocab_ids[None, :]).astype(jnp.bfloat16)
    embedded = jnp.dot(one_hot, embed_table, preferred_element_type=jnp.float32).astype(
        jnp.bfloat16
    )

    def first_hook(full):
        full, pair = after_first_gather(full)
        later["wt_own"] = pair[0]
        return full, pair

    first_mine = section_step(
        embedded,
        core == 0,
        (w_own, w_first),
        of_section(core, feat_own, feat_other, 0),
        padded_se,
        first_hook,
        of_section(core, gain_own, gain_other, 0),
        False,
    )
    second_mine = section_step(
        first_mine,
        core == 1,
        (w_own, later["w"]),
        of_section(core, feat_own, feat_other, 1),
        mr_taps,
        after_second_gather,
        of_section(core, gain_own, gain_other, 1),
        True,
    )

    second_slice_of_first = lax.ppermute(first_mine, "pipe", [(1, 0)])
    first_slice_of_second = lax.ppermute(second_mine, "pipe", [(0, 1)])
    lead = core == 0
    slice_zero = jnp.where(lead, first_mine, first_slice_of_second)
    slice_one = jnp.where(lead, second_slice_of_first, second_mine)
    return jnp.stack([slice_zero, slice_one], axis=0)[None]


def solution(mesh):
    return jax.shard_map(
        local,
        mesh=mesh,
        in_specs=(
            P(None, "seq"),
            P(None, "tensor"),
            P("pipe", None, None, "tensor"),
            P("pipe", None, None, "tensor"),
            P(None, "tensor"),
            P(None, "tensor"),
            P("pipe", "tensor", None),
            P("pipe", "tensor"),
        ),
        out_specs=P("pipe", None, "seq", "tensor"),
        check_vma=False,
    )
```

```python
import jax
import jax.numpy as jnp
from jax import lax
from jax.sharding import PartitionSpec as P

VOCAB = 512
KL = 128
KS = 7
KF = 3
HALO = KL + KF - 2
TY = 4


epsilon = 1e-06


def swapped(value):
    return lax.ppermute(value, "pipe", [(0, 1), (1, 0)])


def of_section(core, own, other, section):
    return jnp.where(core == section, own, other)


def grid_shape():
    n_t = lax.axis_size("tensor")
    return n_t // TY, TY


def shift_pairs(shift_z, shift_y):
    n_z, n_y = grid_shape()
    return [
        (z * n_y + y, ((z + shift_z) % n_z) * n_y + (y + shift_y) % n_y)
        for z in range(n_z)
        for y in range(n_y)
    ]


def ring_gather(block, two_rounds=False):
    n_z, n_y = grid_shape()
    from_below = lax.ppermute(block, "tensor", shift_pairs(0, 1))
    from_above = lax.ppermute(block, "tensor", shift_pairs(0, -1))
    from_two = lax.ppermute(block, "tensor", shift_pairs(0, 2))
    column = jnp.stack([block, from_above, from_two, from_below])
    if two_rounds and n_z == 8:
        near = {a: lax.ppermute(column, "tensor", shift_pairs(-a, 0)) for a in (1, 2, -1, -2)}
        lower = lax.ppermute(jnp.stack([near[-1], near[-2]]), "tensor", shift_pairs(2, 0))
        upper = lax.ppermute(near[1], "tensor", shift_pairs(-2, 0))
        parts = [column, near[1], near[2], upper, lower[1], lower[0], near[-2], near[-1]]
        return jnp.stack(parts)
    ahead, behind = {}, {}
    going_up, going_down = column, column
    for step in range(1, n_z // 2 + 1):
        going_up = lax.ppermute(going_up, "tensor", shift_pairs(1, 0))
        behind[step] = going_up
        if step < n_z - step:
            going_down = lax.ppermute(going_down, "tensor", shift_pairs(-1, 0))
            ahead[step] = going_down
    parts = [column] + [ahead[a] if a in ahead else behind[n_z - a] for a in range(1, n_z)]
    return jnp.stack(parts)


def absolute_order(gathered, flat=False):
    n_z, n_y = grid_shape()
    t = lax.axis_index("tensor")
    z, y = t // n_y, t % n_y
    if flat:
        slots = jnp.arange(n_z * n_y)
        source = ((slots // n_y - z) % n_z) * n_y + (slots % n_y - y) % n_y
        picked = jnp.take(gathered.reshape((n_z * n_y,) + gathered.shape[2:]), source, axis=0, mode="clip")
        return picked.reshape(gathered.shape)
    gathered = jnp.take(gathered, (jnp.arange(n_z) - z) % n_z, axis=0)
    return jnp.take(gathered, (jnp.arange(n_y) - y) % n_y, axis=1)


def chosen_dot(use_own, spec, lhs, own, other):
    return lax.cond(
        use_own,
        lambda a, w, _: jnp.einsum(spec, a, w, preferred_element_type=jnp.float32),
        lambda a, _, w: jnp.einsum(spec, a, w, preferred_element_type=jnp.float32),
        lhs,
        own,
        other,
    )


def relaid_out_proj(w_down):
    n_t = lax.axis_size("tensor")
    chan_local, width = w_down.shape
    blocks = w_down.reshape(chan_local, n_t, width // n_t)
    moved = lax.all_to_all(blocks, "tensor", 1, 0, tiled=True)
    return moved.reshape(n_t * chan_local, width // n_t)


def section_step(x_in, use_own, w_in, feat, long_taps, w_out, gain, later=False):
    rows = x_in.shape[0]
    n_z, n_y = grid_shape()
    chan_local = w_in[0].shape[-1]
    aug = jnp.concatenate([x_in, gain.reshape(1, -1).astype(x_in.dtype)], axis=0)
    full, w_out = w_out(ring_gather(aug))
    full = absolute_order(full, later)
    values = full[:, :, :rows].astype(jnp.float32)
    gain_all = full[:, :, rows:].astype(jnp.float32)
    inv_rms = lax.rsqrt(jnp.mean(values * values, axis=(0, 1, 3), keepdims=True) + epsilon)
    normed = (values * inv_rms * gain_all).astype(jnp.bfloat16)
    w_grid = [w.reshape((n_z, n_y, -1) + w.shape[1:]) for w in w_in]
    projected = chosen_dot(use_own, "abrf,abfjc->rjc", normed, *w_grid).astype(jnp.bfloat16)

    blocks = lax.axis_size("pipe") * lax.axis_size("seq")
    tail = lax.ppermute(
        projected[rows - HALO :], ("pipe", "seq"), [(b, b + 1) for b in range(blocks - 1)]
    )
    kv_prev = tail[:, 1:]
    q_prev = tail[HALO - (KF - 1) :, 0]

    q_all = jnp.concatenate([q_prev, projected[:, 0]], axis=0).astype(jnp.float32)
    kv_all = jnp.concatenate([kv_prev, projected[:, 1:]], axis=0).astype(jnp.float32)
    q_taps = feat[:, 0, :]
    kv_taps = feat[:, 1:, :]
    kv_span = KL - 1 + rows
    q_feat = jnp.zeros((rows, chan_local), jnp.float32)
    kv_feat = jnp.zeros((kv_span, 2, chan_local), jnp.float32)
    for tap_index in range(KF):
        offset = KF - 1 - tap_index
        q_feat = q_feat + q_taps[tap_index] * q_all[offset : offset + rows]
        kv_feat = kv_feat + kv_taps[tap_index] * kv_all[offset : offset + kv_span]
    gated_kv = kv_feat[:, 0] * kv_feat[:, 1]

    filtered = jnp.zeros_like(q_feat)
    for tap_index in range(KL):
        start = KL - 1 - tap_index
        filtered = filtered + long_taps[tap_index] * gated_kv[start : start + rows]
    y_out = (q_feat * filtered).astype(jnp.bfloat16)
    y_full = absolute_order(ring_gather(y_out, later), later)
    w_out_grid = [w.reshape((n_z, n_y, -1, w.shape[-1])) for w in w_out]
    mixed = chosen_dot(use_own, "abrc,abcd->rd", y_full, *w_out_grid)
    return (x_in.astype(jnp.float32) + mixed).astype(jnp.bfloat16)


def local(token_ids, embed_table, in_proj, feat_taps, se_taps, mr_taps, out_proj, norm_gain):
    core = lax.axis_index("pipe")

    w_own = in_proj[0]
    feat_own = feat_taps[0]
    gain_own = norm_gain[0]
    w_other, feat_other, gain_other = swapped((w_own, feat_own, gain_own))

    def out_weights_after(full):
        full, w_down = lax.optimization_barrier((full, out_proj[0]))
        wt_own = relaid_out_proj(w_down)
        return full, (wt_own, swapped(wt_own))

    padded_se = jnp.concatenate(
        [se_taps, jnp.zeros((KL - KS, se_taps.shape[1]), jnp.float32)], axis=0
    )
    filters = (padded_se, mr_taps)

    ids = lax.dynamic_index_in_dim(token_ids, core, 0, keepdims=False)
    vocab_ids = jnp.arange(VOCAB, dtype=jnp.int32)
    one_hot = (ids[:, None] == vocab_ids[None, :]).astype(jnp.bfloat16)
    current = jnp.dot(one_hot, embed_table, preferred_element_type=jnp.float32).astype(
        jnp.bfloat16
    )

    results = []
    relaid = []

    def relaid_once(full):
        if relaid:
            return full, relaid
        full, pair = out_weights_after(full)
        relaid.extend(pair)
        return full, pair

    for section in range(2):
        current = section_step(
            current,
            core == section,
            (w_own, w_other),
            of_section(core, feat_own, feat_other, section),
            filters[section],
            relaid_once,
            of_section(core, gain_own, gain_other, section),
            section == 1,
        )
        results.append(current)

    first_mine, second_mine = results
    second_slice_of_first = lax.ppermute(first_mine, "pipe", [(1, 0)])
    first_slice_of_second = lax.ppermute(second_mine, "pipe", [(0, 1)])
    lead = core == 0
    slice_zero = jnp.where(lead, first_mine, first_slice_of_second)
    slice_one = jnp.where(lead, second_slice_of_first, second_mine)
    return jnp.stack([slice_zero, slice_one], axis=0)[None]


def solution(mesh):
    return jax.shard_map(
        local,
        mesh=mesh,
        in_specs=(
            P(None, "seq"),
            P(None, "tensor"),
            P("pipe", None, None, "tensor"),
            P("pipe", None, None, "tensor"),
            P(None, "tensor"),
            P(None, "tensor"),
            P("pipe", "tensor", None),
            P("pipe", "tensor"),
        ),
        out_specs=P("pipe", None, "seq", "tensor"),
        check_vma=False,
    )
```

```python
import jax
import jax.numpy as jnp
from jax import lax
from jax.sharding import PartitionSpec as P

VOCAB = 512
KL = 128
KS = 7
KF = 3
HALO = KL + KF - 2
TY = 4


epsilon = 1e-06


def swapped(value):
    return lax.ppermute(value, "pipe", [(0, 1), (1, 0)])


def of_section(core, own, other, section):
    return jnp.where(core == section, own, other)


def grid_shape():
    n_t = lax.axis_size("tensor")
    return n_t // TY, TY


def shift_pairs(shift_z, shift_y):
    n_z, n_y = grid_shape()
    return [
        (z * n_y + y, ((z + shift_z) % n_z) * n_y + (y + shift_y) % n_y)
        for z in range(n_z)
        for y in range(n_y)
    ]


def ring_gather(block, two_rounds=False):
    n_z, n_y = grid_shape()
    from_below = lax.ppermute(block, "tensor", shift_pairs(0, 1))
    from_above = lax.ppermute(block, "tensor", shift_pairs(0, -1))
    from_two = lax.ppermute(block, "tensor", shift_pairs(0, 2))
    column = jnp.stack([block, from_above, from_two, from_below])
    if two_rounds and n_z == 8:
        near = {a: lax.ppermute(column, "tensor", shift_pairs(-a, 0)) for a in (1, 2, -1, -2)}
        lower = lax.ppermute(jnp.stack([near[-1], near[-2]]), "tensor", shift_pairs(2, 0))
        upper = lax.ppermute(near[1], "tensor", shift_pairs(-2, 0))
        parts = [column, near[1], near[2], upper, lower[1], lower[0], near[-2], near[-1]]
        return jnp.stack(parts)
    ahead, behind = {}, {}
    going_up, going_down = column, column
    for step in range(1, n_z // 2 + 1):
        going_up = lax.ppermute(going_up, "tensor", shift_pairs(1, 0))
        behind[step] = going_up
        if step < n_z - step:
            going_down = lax.ppermute(going_down, "tensor", shift_pairs(-1, 0))
            ahead[step] = going_down
    parts = [column] + [ahead[a] if a in ahead else behind[n_z - a] for a in range(1, n_z)]
    return jnp.stack(parts)


def absolute_order(gathered, flat=False):
    n_z, n_y = grid_shape()
    t = lax.axis_index("tensor")
    z, y = t // n_y, t % n_y
    if flat:
        slots = jnp.arange(n_z * n_y)
        source = ((slots // n_y - z) % n_z) * n_y + (slots % n_y - y) % n_y
        picked = jnp.take(gathered.reshape((n_z * n_y,) + gathered.shape[2:]), source, axis=0, mode="clip")
        return picked.reshape(gathered.shape)
    gathered = jnp.take(gathered, (jnp.arange(n_z) - z) % n_z, axis=0)
    return jnp.take(gathered, (jnp.arange(n_y) - y) % n_y, axis=1)


def chosen_dot(use_own, spec, lhs, own, other):
    return lax.cond(
        use_own,
        lambda a, w, _: jnp.einsum(spec, a, w, preferred_element_type=jnp.float32),
        lambda a, _, w: jnp.einsum(spec, a, w, preferred_element_type=jnp.float32),
        lhs,
        own,
        other,
    )


def relaid_out_proj(w_down):
    n_t = lax.axis_size("tensor")
    chan_local, width = w_down.shape
    blocks = w_down.reshape(chan_local, n_t, width // n_t)
    moved = lax.all_to_all(blocks, "tensor", 1, 0, tiled=True)
    return moved.reshape(n_t * chan_local, width // n_t)


def section_step(x_in, use_own, w_in, feat, long_taps, w_out, gain, later=False):
    rows = x_in.shape[0]
    n_z, n_y = grid_shape()
    chan_local = w_in[0].shape[-1]
    aug = jnp.concatenate([x_in, gain.reshape(1, -1).astype(x_in.dtype)], axis=0)
    full, w_out = w_out(ring_gather(aug))
    full = absolute_order(full, True)
    values = full[:, :, :rows].astype(jnp.float32)
    gain_all = full[:, :, rows:].astype(jnp.float32)
    inv_rms = lax.rsqrt(jnp.mean(values * values, axis=(0, 1, 3), keepdims=True) + epsilon)
    normed = (values * inv_rms * gain_all).astype(jnp.bfloat16)
    w_grid = [w.reshape((n_z, n_y, -1) + w.shape[1:]) for w in w_in]
    projected = chosen_dot(use_own, "abrf,abfjc->rjc", normed, *w_grid).astype(jnp.bfloat16)

    blocks = lax.axis_size("pipe") * lax.axis_size("seq")
    tail = lax.ppermute(
        projected[rows - HALO :], ("pipe", "seq"), [(b, b + 1) for b in range(blocks - 1)]
    )
    kv_prev = tail[:, 1:]
    q_prev = tail[HALO - (KF - 1) :, 0]

    q_all = jnp.concatenate([q_prev, projected[:, 0]], axis=0).astype(jnp.float32)
    kv_all = jnp.concatenate([kv_prev, projected[:, 1:]], axis=0).astype(jnp.float32)
    q_taps = feat[:, 0, :]
    kv_taps = feat[:, 1:, :]
    kv_span = KL - 1 + rows
    q_feat = jnp.zeros((rows, chan_local), jnp.float32)
    kv_feat = jnp.zeros((kv_span, 2, chan_local), jnp.float32)
    for tap_index in range(KF):
        offset = KF - 1 - tap_index
        q_feat = q_feat + q_taps[tap_index] * q_all[offset : offset + rows]
        kv_feat = kv_feat + kv_taps[tap_index] * kv_all[offset : offset + kv_span]
    gated_kv = kv_feat[:, 0] * kv_feat[:, 1]

    filtered = jnp.zeros_like(q_feat)
    for tap_index in range(KL):
        start = KL - 1 - tap_index
        filtered = filtered + long_taps[tap_index] * gated_kv[start : start + rows]
    y_out = (q_feat * filtered).astype(jnp.bfloat16)
    y_full = absolute_order(ring_gather(y_out, later), later)
    w_out_grid = [w.reshape((n_z, n_y, -1, w.shape[-1])) for w in w_out]
    mixed = chosen_dot(use_own, "abrc,abcd->rd", y_full, *w_out_grid)
    return (x_in.astype(jnp.float32) + mixed).astype(jnp.bfloat16)


def local(token_ids, embed_table, in_proj, feat_taps, se_taps, mr_taps, out_proj, norm_gain):
    core = lax.axis_index("pipe")

    w_own = in_proj[0]
    feat_own = feat_taps[0]
    gain_own = norm_gain[0]
    w_other, feat_other, gain_other = swapped((w_own, feat_own, gain_own))

    def out_weights_after(full):
        full, w_down = lax.optimization_barrier((full, out_proj[0]))
        wt_own = relaid_out_proj(w_down)
        return full, (wt_own, swapped(wt_own))

    padded_se = jnp.concatenate(
        [se_taps, jnp.zeros((KL - KS, se_taps.shape[1]), jnp.float32)], axis=0
    )
    filters = (padded_se, mr_taps)

    ids = lax.dynamic_index_in_dim(token_ids, core, 0, keepdims=False)
    vocab_ids = jnp.arange(VOCAB, dtype=jnp.int32)
    one_hot = (ids[:, None] == vocab_ids[None, :]).astype(jnp.bfloat16)
    current = jnp.dot(one_hot, embed_table, preferred_element_type=jnp.float32).astype(
        jnp.bfloat16
    )

    results = []
    relaid = []

    def relaid_once(full):
        if relaid:
            return full, relaid
        full, pair = out_weights_after(full)
        relaid.extend(pair)
        return full, pair

    for section in range(2):
        current = section_step(
            current,
            core == section,
            (w_own, w_other),
            of_section(core, feat_own, feat_other, section),
            filters[section],
            relaid_once,
            of_section(core, gain_own, gain_other, section),
            section == 1,
        )
        results.append(current)

    first_mine, second_mine = results
    second_slice_of_first = lax.ppermute(first_mine, "pipe", [(1, 0)])
    first_slice_of_second = lax.ppermute(second_mine, "pipe", [(0, 1)])
    lead = core == 0
    slice_zero = jnp.where(lead, first_mine, first_slice_of_second)
    slice_one = jnp.where(lead, second_slice_of_first, second_mine)
    return jnp.stack([slice_zero, slice_one], axis=0)[None]


def solution(mesh):
    return jax.shard_map(
        local,
        mesh=mesh,
        in_specs=(
            P(None, "seq"),
            P(None, "tensor"),
            P("pipe", None, None, "tensor"),
            P("pipe", None, None, "tensor"),
            P(None, "tensor"),
            P(None, "tensor"),
            P("pipe", "tensor", None),
            P("pipe", "tensor"),
        ),
        out_specs=P("pipe", None, "seq", "tensor"),
        check_vma=False,
    )
```

```python
import jax
import jax.numpy as jnp
from jax import lax
from jax.sharding import PartitionSpec as P

VOCAB = 512
KL = 128
KS = 7
KF = 3
HALO = KL + KF - 2
TY = 4


epsilon = 1e-06


def swapped(value):
    return lax.ppermute(value, "pipe", [(0, 1), (1, 0)])


def of_section(core, own, other, section):
    return jnp.where(core == section, own, other)


def grid_shape():
    n_t = lax.axis_size("tensor")
    return n_t // TY, TY


def shift_pairs(shift_z, shift_y):
    n_z, n_y = grid_shape()
    return [
        (z * n_y + y, ((z + shift_z) % n_z) * n_y + (y + shift_y) % n_y)
        for z in range(n_z)
        for y in range(n_y)
    ]


def ring_gather(block, two_rounds=False):
    n_z, n_y = grid_shape()
    from_below = lax.ppermute(block, "tensor", shift_pairs(0, 1))
    from_above = lax.ppermute(block, "tensor", shift_pairs(0, -1))
    from_two = lax.ppermute(block, "tensor", shift_pairs(0, 2))
    column = jnp.stack([block, from_above, from_two, from_below])
    if two_rounds and n_z == 8:
        near = {a: lax.ppermute(column, "tensor", shift_pairs(-a, 0)) for a in (1, 2, -1, -2)}
        lower = lax.ppermute(jnp.stack([near[-1], near[-2]]), "tensor", shift_pairs(2, 0))
        upper = lax.ppermute(near[1], "tensor", shift_pairs(-2, 0))
        parts = [column, near[1], near[2], upper, lower[1], lower[0], near[-2], near[-1]]
        return jnp.stack(parts)
    ahead, behind = {}, {}
    going_up, going_down = column, column
    for step in range(1, n_z // 2 + 1):
        going_up = lax.ppermute(going_up, "tensor", shift_pairs(1, 0))
        behind[step] = going_up
        if step < n_z - step:
            going_down = lax.ppermute(going_down, "tensor", shift_pairs(-1, 0))
            ahead[step] = going_down
    parts = [column] + [ahead[a] if a in ahead else behind[n_z - a] for a in range(1, n_z)]
    return jnp.stack(parts)


def absolute_order(gathered, flat=False):
    n_z, n_y = grid_shape()
    t = lax.axis_index("tensor")
    z, y = t // n_y, t % n_y
    if flat:
        slots = jnp.arange(n_z * n_y)
        source = ((slots // n_y - z) % n_z) * n_y + (slots % n_y - y) % n_y
        picked = jnp.take(gathered.reshape((n_z * n_y,) + gathered.shape[2:]), source, axis=0, mode="clip")
        return picked.reshape(gathered.shape)
    gathered = jnp.take(gathered, (jnp.arange(n_z) - z) % n_z, axis=0)
    return jnp.take(gathered, (jnp.arange(n_y) - y) % n_y, axis=1)


def chosen_dot(use_own, spec, lhs, own, other):
    return lax.cond(
        use_own,
        lambda a, w, _: jnp.einsum(spec, a, w, preferred_element_type=jnp.float32),
        lambda a, _, w: jnp.einsum(spec, a, w, preferred_element_type=jnp.float32),
        lhs,
        own,
        other,
    )


def relaid_out_proj(w_down):
    n_t = lax.axis_size("tensor")
    n_x = lax.axis_size("seq")
    x = lax.axis_index("seq")
    chan_local, width = w_down.shape
    share = chan_local // n_x
    mine = lax.dynamic_slice_in_dim(w_down, x * share, share, 0)
    blocks = mine.reshape(share, n_t, width // n_t)
    moved = lax.all_to_all(blocks, "tensor", 1, 0, tiled=True).reshape(n_t, share, width // n_t)
    quarters = [moved] + [
        lax.ppermute(moved, "seq", [(i, (i - s) % n_x) for i in range(n_x)]) for s in range(1, n_x)
    ]
    stacked = jnp.stack(quarters)
    stacked = jnp.take(stacked, (jnp.arange(n_x) - x) % n_x, axis=0, mode="clip")
    return jnp.transpose(stacked, (1, 0, 2, 3)).reshape(n_t * chan_local, width // n_t)


def section_step(x_in, use_own, w_in, feat, long_taps, w_out, gain, later=False):
    rows = x_in.shape[0]
    n_z, n_y = grid_shape()
    chan_local = w_in[0].shape[-1]
    aug = jnp.concatenate([x_in, gain.reshape(1, -1).astype(x_in.dtype)], axis=0)
    full, w_out = w_out(ring_gather(aug))
    full = absolute_order(full, True)
    values = full[:, :, :rows].astype(jnp.float32)
    gain_all = full[:, :, rows:].astype(jnp.float32)
    inv_rms = lax.rsqrt(jnp.mean(values * values, axis=(0, 1, 3), keepdims=True) + epsilon)
    normed = (values * inv_rms * gain_all).astype(jnp.bfloat16)
    w_grid = [w.reshape((n_z, n_y, -1) + w.shape[1:]) for w in w_in]
    projected = chosen_dot(use_own, "abrf,abfjc->rjc", normed, *w_grid).astype(jnp.bfloat16)

    blocks = lax.axis_size("pipe") * lax.axis_size("seq")
    tail = lax.ppermute(
        projected[rows - HALO :], ("pipe", "seq"), [(b, b + 1) for b in range(blocks - 1)]
    )
    kv_prev = tail[:, 1:]
    q_prev = tail[HALO - (KF - 1) :, 0]

    q_all = jnp.concatenate([q_prev, projected[:, 0]], axis=0).astype(jnp.float32)
    kv_all = jnp.concatenate([kv_prev, projected[:, 1:]], axis=0).astype(jnp.float32)
    q_taps = feat[:, 0, :]
    kv_taps = feat[:, 1:, :]
    kv_span = KL - 1 + rows
    q_feat = jnp.zeros((rows, chan_local), jnp.float32)
    kv_feat = jnp.zeros((kv_span, 2, chan_local), jnp.float32)
    for tap_index in range(KF):
        offset = KF - 1 - tap_index
        q_feat = q_feat + q_taps[tap_index] * q_all[offset : offset + rows]
        kv_feat = kv_feat + kv_taps[tap_index] * kv_all[offset : offset + kv_span]
    gated_kv = kv_feat[:, 0] * kv_feat[:, 1]

    filtered = jnp.zeros_like(q_feat)
    for tap_index in range(KL):
        start = KL - 1 - tap_index
        filtered = filtered + long_taps[tap_index] * gated_kv[start : start + rows]
    y_out = (q_feat * filtered).astype(jnp.bfloat16)
    y_full = absolute_order(ring_gather(y_out, later), later)
    w_out_grid = [w.reshape((n_z, n_y, -1, w.shape[-1])) for w in w_out]
    mixed = chosen_dot(use_own, "abrc,abcd->rd", y_full, *w_out_grid)
    return (x_in.astype(jnp.float32) + mixed).astype(jnp.bfloat16)


def local(token_ids, embed_table, in_proj, feat_taps, se_taps, mr_taps, out_proj, norm_gain):
    core = lax.axis_index("pipe")

    w_own = in_proj[0]
    feat_own = feat_taps[0]
    gain_own = norm_gain[0]
    w_other, feat_other, gain_other = swapped((w_own, feat_own, gain_own))

    def out_weights_after(full):
        full, w_down = lax.optimization_barrier((full, out_proj[0]))
        wt_own = relaid_out_proj(w_down)
        return full, (wt_own, swapped(wt_own))

    padded_se = jnp.concatenate(
        [se_taps, jnp.zeros((KL - KS, se_taps.shape[1]), jnp.float32)], axis=0
    )
    filters = (padded_se, mr_taps)

    ids = lax.dynamic_index_in_dim(token_ids, core, 0, keepdims=False)
    vocab_ids = jnp.arange(VOCAB, dtype=jnp.int32)
    one_hot = (ids[:, None] == vocab_ids[None, :]).astype(jnp.bfloat16)
    current = jnp.dot(one_hot, embed_table, preferred_element_type=jnp.float32).astype(
        jnp.bfloat16
    )

    results = []
    relaid = []

    def relaid_once(full):
        if relaid:
            return full, relaid
        full, pair = out_weights_after(full)
        relaid.extend(pair)
        return full, pair

    for section in range(2):
        current = section_step(
            current,
            core == section,
            (w_own, w_other),
            of_section(core, feat_own, feat_other, section),
            filters[section],
            relaid_once,
            of_section(core, gain_own, gain_other, section),
            section == 1,
        )
        results.append(current)

    first_mine, second_mine = results
    second_slice_of_first = lax.ppermute(first_mine, "pipe", [(1, 0)])
    first_slice_of_second = lax.ppermute(second_mine, "pipe", [(0, 1)])
    lead = core == 0
    slice_zero = jnp.where(lead, first_mine, first_slice_of_second)
    slice_one = jnp.where(lead, second_slice_of_first, second_mine)
    return jnp.stack([slice_zero, slice_one], axis=0)[None]


def solution(mesh):
    return jax.shard_map(
        local,
        mesh=mesh,
        in_specs=(
            P(None, "seq"),
            P(None, "tensor"),
            P("pipe", None, None, "tensor"),
            P("pipe", None, None, "tensor"),
            P(None, "tensor"),
            P(None, "tensor"),
            P("pipe", "tensor", None),
            P("pipe", "tensor"),
        ),
        out_specs=P("pipe", None, "seq", "tensor"),
        check_vma=False,
    )
```

```python
import jax
import jax.numpy as jnp
from jax import lax
from jax.sharding import PartitionSpec as P

VOCAB = 512
KL = 128
KS = 7
KF = 3
HALO = KL + KF - 2
TY = 4


epsilon = 1e-06


def swapped(value):
    return lax.ppermute(value, "pipe", [(0, 1), (1, 0)])


def of_section(core, own, other, section):
    return jnp.where(core == section, own, other)


def grid_shape():
    n_t = lax.axis_size("tensor")
    return n_t // TY, TY


def shift_pairs(shift_z, shift_y):
    n_z, n_y = grid_shape()
    return [
        (z * n_y + y, ((z + shift_z) % n_z) * n_y + (y + shift_y) % n_y)
        for z in range(n_z)
        for y in range(n_y)
    ]


def ring_gather(block, two_rounds=False):
    n_z, n_y = grid_shape()
    from_below = lax.ppermute(block, "tensor", shift_pairs(0, 1))
    from_above = lax.ppermute(block, "tensor", shift_pairs(0, -1))
    from_two = lax.ppermute(block, "tensor", shift_pairs(0, 2))
    column = jnp.stack([block, from_above, from_two, from_below])
    if two_rounds and n_z == 8:
        near = {a: lax.ppermute(column, "tensor", shift_pairs(-a, 0)) for a in (1, 2, -1, -2)}
        lower = lax.ppermute(jnp.stack([near[-1], near[-2]]), "tensor", shift_pairs(2, 0))
        upper = lax.ppermute(near[1], "tensor", shift_pairs(-2, 0))
        parts = [column, near[1], near[2], upper, lower[1], lower[0], near[-2], near[-1]]
        return jnp.stack(parts)
    ahead, behind = {}, {}
    going_up, going_down = column, column
    for step in range(1, n_z // 2 + 1):
        going_up = lax.ppermute(going_up, "tensor", shift_pairs(1, 0))
        behind[step] = going_up
        if step < n_z - step:
            going_down = lax.ppermute(going_down, "tensor", shift_pairs(-1, 0))
            ahead[step] = going_down
    parts = [column] + [ahead[a] if a in ahead else behind[n_z - a] for a in range(1, n_z)]
    return jnp.stack(parts)


def absolute_order(gathered, flat=False):
    n_z, n_y = grid_shape()
    t = lax.axis_index("tensor")
    z, y = t // n_y, t % n_y
    if flat:
        slots = jnp.arange(n_z * n_y)
        source = ((slots // n_y - z) % n_z) * n_y + (slots % n_y - y) % n_y
        picked = jnp.take(gathered.reshape((n_z * n_y,) + gathered.shape[2:]), source, axis=0, mode="clip")
        return picked.reshape(gathered.shape)
    gathered = jnp.take(gathered, (jnp.arange(n_z) - z) % n_z, axis=0)
    return jnp.take(gathered, (jnp.arange(n_y) - y) % n_y, axis=1)


def chosen_dot(use_own, spec, lhs, own, other):
    return lax.cond(
        use_own,
        lambda a, w, _: jnp.einsum(spec, a, w, preferred_element_type=jnp.float32),
        lambda a, _, w: jnp.einsum(spec, a, w, preferred_element_type=jnp.float32),
        lhs,
        own,
        other,
    )


def quarter_moved(w_down):
    n_t = lax.axis_size("tensor")
    n_x = lax.axis_size("seq")
    chan_local, width = w_down.shape
    share = chan_local // n_x
    mine = lax.dynamic_slice_in_dim(w_down, lax.axis_index("seq") * share, share, 0)
    blocks = mine.reshape(share, n_t, width // n_t)
    return lax.all_to_all(blocks, "tensor", 1, 0, tiled=True).reshape(n_t, share, width // n_t)


def shared_quarters(moved):
    n_x = lax.axis_size("seq")
    x = lax.axis_index("seq")
    quarters = [moved] + [
        lax.ppermute(moved, "seq", [(i, (i - s) % n_x) for i in range(n_x)]) for s in range(1, n_x)
    ]
    stacked = jnp.take(jnp.stack(quarters), (jnp.arange(n_x) - x) % n_x, axis=0, mode="clip")
    n_t, share, cols = moved.shape
    return jnp.transpose(stacked, (1, 0, 2, 3)).reshape(n_t * n_x * share, cols)


def section_step(x_in, use_own, w_in, feat, long_taps, w_out, gain, later=False):
    rows = x_in.shape[0]
    n_z, n_y = grid_shape()
    chan_local = w_in[0].shape[-1]
    aug = jnp.concatenate([x_in, gain.reshape(1, -1).astype(x_in.dtype)], axis=0)
    full, w_out = w_out(ring_gather(aug))
    full = absolute_order(full, later)
    values = full[:, :, :rows].astype(jnp.float32)
    gain_all = full[:, :, rows:].astype(jnp.float32)
    inv_rms = lax.rsqrt(jnp.mean(values * values, axis=(0, 1, 3), keepdims=True) + epsilon)
    normed = (values * inv_rms * gain_all).astype(jnp.bfloat16)
    w_grid = [w.reshape((n_z, n_y, -1) + w.shape[1:]) for w in w_in]
    projected = chosen_dot(use_own, "abrf,abfjc->rjc", normed, *w_grid).astype(jnp.bfloat16)

    blocks = lax.axis_size("pipe") * lax.axis_size("seq")
    tail = lax.ppermute(
        projected[rows - HALO :], ("pipe", "seq"), [(b, b + 1) for b in range(blocks - 1)]
    )
    tail, w_out = w_out(tail)
    kv_prev = tail[:, 1:]
    q_prev = tail[HALO - (KF - 1) :, 0]

    q_all = jnp.concatenate([q_prev, projected[:, 0]], axis=0).astype(jnp.float32)
    kv_all = jnp.concatenate([kv_prev, projected[:, 1:]], axis=0).astype(jnp.float32)
    q_taps = feat[:, 0, :]
    kv_taps = feat[:, 1:, :]
    kv_span = KL - 1 + rows
    q_feat = jnp.zeros((rows, chan_local), jnp.float32)
    kv_feat = jnp.zeros((kv_span, 2, chan_local), jnp.float32)
    for tap_index in range(KF):
        offset = KF - 1 - tap_index
        q_feat = q_feat + q_taps[tap_index] * q_all[offset : offset + rows]
        kv_feat = kv_feat + kv_taps[tap_index] * kv_all[offset : offset + kv_span]
    gated_kv = kv_feat[:, 0] * kv_feat[:, 1]

    filtered = jnp.zeros_like(q_feat)
    for tap_index in range(KL):
        start = KL - 1 - tap_index
        filtered = filtered + long_taps[tap_index] * gated_kv[start : start + rows]
    y_out = (q_feat * filtered).astype(jnp.bfloat16)
    y_full = absolute_order(ring_gather(y_out, later), later)
    w_out_grid = [w.reshape((n_z, n_y, -1, w.shape[-1])) for w in w_out]
    mixed = chosen_dot(use_own, "abrc,abcd->rd", y_full, *w_out_grid)
    return (x_in.astype(jnp.float32) + mixed).astype(jnp.bfloat16)


def local(token_ids, embed_table, in_proj, feat_taps, se_taps, mr_taps, out_proj, norm_gain):
    core = lax.axis_index("pipe")

    w_own = in_proj[0]
    feat_own = feat_taps[0]
    gain_own = norm_gain[0]
    w_other, feat_other, gain_other = swapped((w_own, feat_own, gain_own))

    relaid = []

    def out_weights_after(full):
        full, w_down = lax.optimization_barrier((full, out_proj[0]))
        moved = quarter_moved(w_down)

        def finish(tail):
            tail, held = lax.optimization_barrier((tail, moved))
            wt_own = shared_quarters(held)
            relaid.extend((wt_own, swapped(wt_own)))
            return tail, tuple(relaid)

        return full, finish

    padded_se = jnp.concatenate(
        [se_taps, jnp.zeros((KL - KS, se_taps.shape[1]), jnp.float32)], axis=0
    )
    filters = (padded_se, mr_taps)

    ids = lax.dynamic_index_in_dim(token_ids, core, 0, keepdims=False)
    vocab_ids = jnp.arange(VOCAB, dtype=jnp.int32)
    one_hot = (ids[:, None] == vocab_ids[None, :]).astype(jnp.bfloat16)
    current = jnp.dot(one_hot, embed_table, preferred_element_type=jnp.float32).astype(
        jnp.bfloat16
    )

    results = []
    def relaid_once(full):
        if relaid:
            return full, lambda tail: (tail, tuple(relaid))
        return out_weights_after(full)

    for section in range(2):
        current = section_step(
            current,
            core == section,
            (w_own, w_other),
            of_section(core, feat_own, feat_other, section),
            filters[section],
            relaid_once,
            of_section(core, gain_own, gain_other, section),
            section == 1,
        )
        results.append(current)

    first_mine, second_mine = results
    second_slice_of_first = lax.ppermute(first_mine, "pipe", [(1, 0)])
    first_slice_of_second = lax.ppermute(second_mine, "pipe", [(0, 1)])
    lead = core == 0
    slice_zero = jnp.where(lead, first_mine, first_slice_of_second)
    slice_one = jnp.where(lead, second_slice_of_first, second_mine)
    return jnp.stack([slice_zero, slice_one], axis=0)[None]


def solution(mesh):
    return jax.shard_map(
        local,
        mesh=mesh,
        in_specs=(
            P(None, "seq"),
            P(None, "tensor"),
            P("pipe", None, None, "tensor"),
            P("pipe", None, None, "tensor"),
            P(None, "tensor"),
            P(None, "tensor"),
            P("pipe", "tensor", None),
            P("pipe", "tensor"),
        ),
        out_specs=P("pipe", None, "seq", "tensor"),
        check_vma=False,
    )
```

```python
import jax
import jax.numpy as jnp
from jax import lax
from jax.sharding import PartitionSpec as P

VOCAB = 512
KL = 128
KS = 7
KF = 3
HALO = KL + KF - 2
TY = 4


epsilon = 1e-06


def swapped(value):
    return lax.ppermute(value, "pipe", [(0, 1), (1, 0)])


def of_section(core, own, other, section):
    return jnp.where(core == section, own, other)


def grid_shape():
    n_t = lax.axis_size("tensor")
    return n_t // TY, TY


def shift_pairs(shift_z, shift_y):
    n_z, n_y = grid_shape()
    return [
        (z * n_y + y, ((z + shift_z) % n_z) * n_y + (y + shift_y) % n_y)
        for z in range(n_z)
        for y in range(n_y)
    ]


def ring_gather(block, two_rounds=False):
    n_z, n_y = grid_shape()
    from_below = lax.ppermute(block, "tensor", shift_pairs(0, 1))
    from_above = lax.ppermute(block, "tensor", shift_pairs(0, -1))
    from_two = lax.ppermute(block, "tensor", shift_pairs(0, 2))
    column = jnp.stack([block, from_above, from_two, from_below])
    if two_rounds and n_z == 8:
        near = {a: lax.ppermute(column, "tensor", shift_pairs(-a, 0)) for a in (1, 2, -1, -2)}
        lower = lax.ppermute(jnp.stack([near[-1], near[-2]]), "tensor", shift_pairs(2, 0))
        upper = lax.ppermute(near[1], "tensor", shift_pairs(-2, 0))
        parts = [column, near[1], near[2], upper, lower[1], lower[0], near[-2], near[-1]]
        return jnp.stack(parts)
    ahead, behind = {}, {}
    going_up, going_down = column, column
    for step in range(1, n_z // 2 + 1):
        going_up = lax.ppermute(going_up, "tensor", shift_pairs(1, 0))
        behind[step] = going_up
        if step < n_z - step:
            going_down = lax.ppermute(going_down, "tensor", shift_pairs(-1, 0))
            ahead[step] = going_down
    parts = [column] + [ahead[a] if a in ahead else behind[n_z - a] for a in range(1, n_z)]
    return jnp.stack(parts)


def absolute_order(gathered, flat=False):
    n_z, n_y = grid_shape()
    t = lax.axis_index("tensor")
    z, y = t // n_y, t % n_y
    if flat:
        slots = jnp.arange(n_z * n_y)
        source = ((slots // n_y - z) % n_z) * n_y + (slots % n_y - y) % n_y
        picked = jnp.take(gathered.reshape((n_z * n_y,) + gathered.shape[2:]), source, axis=0, mode="clip")
        return picked.reshape(gathered.shape)
    gathered = jnp.take(gathered, (jnp.arange(n_z) - z) % n_z, axis=0)
    return jnp.take(gathered, (jnp.arange(n_y) - y) % n_y, axis=1)


def chosen_dot(use_own, spec, lhs, own, other):
    return lax.cond(
        use_own,
        lambda a, w, _: jnp.einsum(spec, a, w, preferred_element_type=jnp.float32),
        lambda a, _, w: jnp.einsum(spec, a, w, preferred_element_type=jnp.float32),
        lhs,
        own,
        other,
    )


def relaid_out_proj(w_down):
    n_t = lax.axis_size("tensor")
    chan_local, width = w_down.shape
    blocks = w_down.reshape(chan_local, n_t, width // n_t)
    moved = lax.all_to_all(blocks, "tensor", 1, 0, tiled=True)
    return moved.reshape(n_t * chan_local, width // n_t)


def section_step(x_in, use_own, w_in, feat, long_taps, w_out, gain, later=False):
    rows = x_in.shape[0]
    n_z, n_y = grid_shape()
    chan_local = w_in[0].shape[-1]
    aug = jnp.concatenate([x_in, gain.reshape(1, -1).astype(x_in.dtype)], axis=0)
    full, w_out = w_out(ring_gather(aug))
    full = absolute_order(full, later)
    values = full[:, :, :rows].astype(jnp.float32)
    gain_all = full[:, :, rows:].astype(jnp.float32)
    inv_rms = lax.rsqrt(jnp.mean(values * values, axis=(0, 1, 3), keepdims=True) + epsilon)
    normed = (values * inv_rms * gain_all).astype(jnp.bfloat16)
    w_grid = [w.reshape((n_z, n_y, -1) + w.shape[1:]) for w in w_in]
    projected = chosen_dot(use_own, "abrf,abfjc->rjc", normed, *w_grid).astype(jnp.bfloat16)

    blocks = lax.axis_size("pipe") * lax.axis_size("seq")
    tail = lax.ppermute(
        projected[rows - HALO :], ("pipe", "seq"), [(b, b + 1) for b in range(blocks - 1)]
    )
    kv_prev = tail[:, 1:]
    q_prev = tail[HALO - (KF - 1) :, 0]

    q_all = jnp.concatenate([q_prev, projected[:, 0]], axis=0).astype(jnp.float32)
    kv_all = jnp.concatenate([kv_prev, projected[:, 1:]], axis=0).astype(jnp.float32)
    q_taps = feat[:, 0, :]
    kv_taps = feat[:, 1:, :]
    kv_span = KL - 1 + rows
    q_feat = jnp.zeros((rows, chan_local), jnp.float32)
    kv_feat = jnp.zeros((kv_span, 2, chan_local), jnp.float32)
    for tap_index in range(KF):
        offset = KF - 1 - tap_index
        q_feat = q_feat + q_taps[tap_index] * q_all[offset : offset + rows]
        kv_feat = kv_feat + kv_taps[tap_index] * kv_all[offset : offset + kv_span]
    gated_kv = kv_feat[:, 0] * kv_feat[:, 1]

    filtered = jnp.zeros_like(q_feat)
    for tap_index in range(KL):
        start = KL - 1 - tap_index
        filtered = filtered + long_taps[tap_index] * gated_kv[start : start + rows]
    y_out = (q_feat * filtered).astype(jnp.bfloat16)
    y_full = absolute_order(ring_gather(y_out, later), later)
    w_out_grid = [w.reshape((n_z, n_y, -1, w.shape[-1])) for w in w_out]
    mixed = chosen_dot(use_own, "abrc,abcd->rd", y_full, *w_out_grid)
    return (x_in.astype(jnp.float32) + mixed).astype(jnp.bfloat16)


def local(token_ids, embed_table, in_proj, feat_taps, se_taps, mr_taps, out_proj, norm_gain):
    core = lax.axis_index("pipe")

    w_own = in_proj[0]
    feat_own = feat_taps[0]
    gain_own = norm_gain[0]
    w_other, feat_other, gain_other = swapped((w_own, feat_own, gain_own))

    def out_weights_after(full):
        full, w_down = lax.optimization_barrier((full, out_proj[0]))
        wt_own = relaid_out_proj(w_down)
        return full, (wt_own, swapped(wt_own))

    padded_se = jnp.concatenate(
        [se_taps, jnp.zeros((KL - KS, se_taps.shape[1]), jnp.float32)], axis=0
    )
    filters = (padded_se, mr_taps)

    ids = lax.dynamic_index_in_dim(token_ids, core, 0, keepdims=False)
    vocab_ids = jnp.arange(VOCAB, dtype=jnp.int32)
    one_hot = (ids[:, None] == vocab_ids[None, :]).astype(jnp.bfloat16)
    current = jnp.dot(one_hot, embed_table, preferred_element_type=jnp.float32).astype(
        jnp.bfloat16
    )

    results = []
    relaid = []

    def relaid_once(full):
        if relaid:
            return full, relaid
        full, pair = out_weights_after(full)
        relaid.extend(pair)
        return full, pair

    for section in range(2):
        if section == 1:
            current, taps = lax.optimization_barrier((current, filters[1]))
            filters = (filters[0], taps)
        current = section_step(
            current,
            core == section,
            (w_own, w_other),
            of_section(core, feat_own, feat_other, section),
            filters[section],
            relaid_once,
            of_section(core, gain_own, gain_other, section),
            section == 1,
        )
        results.append(current)

    first_mine, second_mine = results
    second_slice_of_first = lax.ppermute(first_mine, "pipe", [(1, 0)])
    first_slice_of_second = lax.ppermute(second_mine, "pipe", [(0, 1)])
    lead = core == 0
    slice_zero = jnp.where(lead, first_mine, first_slice_of_second)
    slice_one = jnp.where(lead, second_slice_of_first, second_mine)
    return jnp.stack([slice_zero, slice_one], axis=0)[None]


def solution(mesh):
    return jax.shard_map(
        local,
        mesh=mesh,
        in_specs=(
            P(None, "seq"),
            P(None, "tensor"),
            P("pipe", None, None, "tensor"),
            P("pipe", None, None, "tensor"),
            P(None, "tensor"),
            P(None, "tensor"),
            P("pipe", "tensor", None),
            P("pipe", "tensor"),
        ),
        out_specs=P("pipe", None, "seq", "tensor"),
        check_vma=False,
    )
```

```python
import jax
import jax.numpy as jnp
from jax import lax
from jax.sharding import PartitionSpec as P

VOCAB = 512
KL = 128
KS = 7
KF = 3
HALO = KL + KF - 2
TY = 4


epsilon = 1e-06


def swapped(value):
    return lax.ppermute(value, "pipe", [(0, 1), (1, 0)])


def of_section(core, own, other, section):
    return jnp.where(core == section, own, other)


def grid_shape():
    n_t = lax.axis_size("tensor")
    return n_t // TY, TY


def shift_pairs(shift_z, shift_y):
    n_z, n_y = grid_shape()
    return [
        (z * n_y + y, ((z + shift_z) % n_z) * n_y + (y + shift_y) % n_y)
        for z in range(n_z)
        for y in range(n_y)
    ]


def ring_gather(block, two_rounds=False):
    n_z, n_y = grid_shape()
    from_below = lax.ppermute(block, "tensor", shift_pairs(0, 1))
    from_above = lax.ppermute(block, "tensor", shift_pairs(0, -1))
    from_two = lax.ppermute(block, "tensor", shift_pairs(0, 2))
    column = jnp.stack([block, from_above, from_two, from_below])
    if two_rounds and n_z == 8:
        near = {a: lax.ppermute(column, "tensor", shift_pairs(-a, 0)) for a in (1, 2, -1, -2)}
        lower = lax.ppermute(jnp.stack([near[-1], near[-2]]), "tensor", shift_pairs(2, 0))
        upper = lax.ppermute(near[1], "tensor", shift_pairs(-2, 0))
        parts = [column, near[1], near[2], upper, lower[1], lower[0], near[-2], near[-1]]
        return jnp.stack(parts)
    ahead, behind = {}, {}
    going_up, going_down = column, column
    for step in range(1, n_z // 2 + 1):
        going_up = lax.ppermute(going_up, "tensor", shift_pairs(1, 0))
        behind[step] = going_up
        if step < n_z - step:
            going_down = lax.ppermute(going_down, "tensor", shift_pairs(-1, 0))
            ahead[step] = going_down
    parts = [column] + [ahead[a] if a in ahead else behind[n_z - a] for a in range(1, n_z)]
    return jnp.stack(parts)


def absolute_order(gathered, flat=False):
    n_z, n_y = grid_shape()
    t = lax.axis_index("tensor")
    z, y = t // n_y, t % n_y
    if flat:
        slots = jnp.arange(n_z * n_y)
        source = ((slots // n_y - z) % n_z) * n_y + (slots % n_y - y) % n_y
        picked = jnp.take(gathered.reshape((n_z * n_y,) + gathered.shape[2:]), source, axis=0, mode="clip")
        return picked.reshape(gathered.shape)
    gathered = jnp.take(gathered, (jnp.arange(n_z) - z) % n_z, axis=0)
    return jnp.take(gathered, (jnp.arange(n_y) - y) % n_y, axis=1)


def chosen_dot(use_own, spec, lhs, own, other):
    return lax.cond(
        use_own,
        lambda a, w, _: jnp.einsum(spec, a, w, preferred_element_type=jnp.float32),
        lambda a, _, w: jnp.einsum(spec, a, w, preferred_element_type=jnp.float32),
        lhs,
        own,
        other,
    )


def relaid_out_proj(w_down):
    n_t = lax.axis_size("tensor")
    chan_local, width = w_down.shape
    blocks = w_down.reshape(chan_local, n_t, width // n_t)
    moved = lax.all_to_all(blocks, "tensor", 1, 0, tiled=True)
    return moved.reshape(n_t * chan_local, width // n_t)


def section_step(x_in, use_own, w_in, feat, long_taps, w_out, gain, later=False):
    rows = x_in.shape[0]
    n_z, n_y = grid_shape()
    chan_local = w_in[0].shape[-1]
    aug = jnp.concatenate([x_in, gain.reshape(1, -1).astype(x_in.dtype)], axis=0)
    full, w_out = w_out(ring_gather(aug, later))
    full = absolute_order(full, later)
    values = full[:, :, :rows].astype(jnp.float32)
    gain_all = full[:, :, rows:].astype(jnp.float32)
    inv_rms = lax.rsqrt(jnp.mean(values * values, axis=(0, 1, 3), keepdims=True) + epsilon)
    normed = (values * inv_rms * gain_all).astype(jnp.bfloat16)
    w_grid = [w.reshape((n_z, n_y, -1) + w.shape[1:]) for w in w_in]
    projected = chosen_dot(use_own, "abrf,abfjc->rjc", normed, *w_grid).astype(jnp.bfloat16)

    blocks = lax.axis_size("pipe") * lax.axis_size("seq")
    tail = lax.ppermute(
        projected[rows - HALO :], ("pipe", "seq"), [(b, b + 1) for b in range(blocks - 1)]
    )
    kv_prev = tail[:, 1:]
    q_prev = tail[HALO - (KF - 1) :, 0]

    q_all = jnp.concatenate([q_prev, projected[:, 0]], axis=0).astype(jnp.float32)
    kv_all = jnp.concatenate([kv_prev, projected[:, 1:]], axis=0).astype(jnp.float32)
    q_taps = feat[:, 0, :]
    kv_taps = feat[:, 1:, :]
    kv_span = KL - 1 + rows
    q_feat = jnp.zeros((rows, chan_local), jnp.float32)
    kv_feat = jnp.zeros((kv_span, 2, chan_local), jnp.float32)
    for tap_index in range(KF):
        offset = KF - 1 - tap_index
        q_feat = q_feat + q_taps[tap_index] * q_all[offset : offset + rows]
        kv_feat = kv_feat + kv_taps[tap_index] * kv_all[offset : offset + kv_span]
    gated_kv = kv_feat[:, 0] * kv_feat[:, 1]

    filtered = jnp.zeros_like(q_feat)
    for tap_index in range(KL):
        start = KL - 1 - tap_index
        filtered = filtered + long_taps[tap_index] * gated_kv[start : start + rows]
    y_out = (q_feat * filtered).astype(jnp.bfloat16)
    y_full = absolute_order(ring_gather(y_out, later), later)
    w_out_grid = [w.reshape((n_z, n_y, -1, w.shape[-1])) for w in w_out]
    mixed = chosen_dot(use_own, "abrc,abcd->rd", y_full, *w_out_grid)
    return (x_in.astype(jnp.float32) + mixed).astype(jnp.bfloat16)


def local(token_ids, embed_table, in_proj, feat_taps, se_taps, mr_taps, out_proj, norm_gain):
    core = lax.axis_index("pipe")

    w_own = in_proj[0]
    feat_own = feat_taps[0]
    gain_own = norm_gain[0]
    w_other, feat_other, gain_other = swapped((w_own, feat_own, gain_own))

    def out_weights_after(full):
        full, w_down = lax.optimization_barrier((full, out_proj[0]))
        wt_own = relaid_out_proj(w_down)
        return full, (wt_own, swapped(wt_own))

    padded_se = jnp.concatenate(
        [se_taps, jnp.zeros((KL - KS, se_taps.shape[1]), jnp.float32)], axis=0
    )
    filters = (padded_se, mr_taps)

    ids = lax.dynamic_index_in_dim(token_ids, core, 0, keepdims=False)
    vocab_ids = jnp.arange(VOCAB, dtype=jnp.int32)
    one_hot = (ids[:, None] == vocab_ids[None, :]).astype(jnp.bfloat16)
    current = jnp.dot(one_hot, embed_table, preferred_element_type=jnp.float32).astype(
        jnp.bfloat16
    )

    results = []
    relaid = []

    def relaid_once(full):
        if relaid:
            return full, relaid
        full, pair = out_weights_after(full)
        relaid.extend(pair)
        return full, pair

    for section in range(2):
        current = section_step(
            current,
            core == section,
            (w_own, w_other),
            of_section(core, feat_own, feat_other, section),
            filters[section],
            relaid_once,
            of_section(core, gain_own, gain_other, section),
            section == 1,
        )
        results.append(current)

    first_mine, second_mine = results
    second_slice_of_first = lax.ppermute(first_mine, "pipe", [(1, 0)])
    first_slice_of_second = lax.ppermute(second_mine, "pipe", [(0, 1)])
    lead = core == 0
    slice_zero = jnp.where(lead, first_mine, first_slice_of_second)
    slice_one = jnp.where(lead, second_slice_of_first, second_mine)
    return jnp.stack([slice_zero, slice_one], axis=0)[None]


def solution(mesh):
    return jax.shard_map(
        local,
        mesh=mesh,
        in_specs=(
            P(None, "seq"),
            P(None, "tensor"),
            P("pipe", None, None, "tensor"),
            P("pipe", None, None, "tensor"),
            P(None, "tensor"),
            P(None, "tensor"),
            P("pipe", "tensor", None),
            P("pipe", "tensor"),
        ),
        out_specs=P("pipe", None, "seq", "tensor"),
        check_vma=False,
    )
```
